32 devices in a mesh: pair: 4 (over z), src: 2 (over x), tgt: 4 (over y, core).
Axes of the slice: x: 2, y: 2, z: 4, core: 2. Of those that a mesh axis runs over, the one named last changes fastest.
Arguments:
- src_cells: float32 [4, 30, 4096], P('pair', None, 'src'), may hold values from -17 to 17
- final_cells: float32 [30, 4096], P(None, 'tgt'), may hold values from -17 to 17
- growth: float32 [4, 4096], P('pair', 'src'), may hold values from 0.5 to 2
- live: int32 [5], replicated, may hold values from 1024 to 4096, as said below
- final_fates: float32 [40, 4096], P(None, 'tgt'), may hold values from 0 to 1
Outputs:
- fate_maps: float32 [4, 40, 4096], P('pair', None, ('src', 'tgt'))
- potentials: float32 [4, 4096], P('pair', 'src')
The draws below stay inside these ranges and needn't reach their ends.
Inputs may be any that keep to these rules, and one draw needn't show every extreme that they name: `live`: every count is at least 1024 and one snapshot fills all 4096 slots.
All inputs are finite; a program needn't handle non-finite values.
Results may differ from the reference program's by a relative error of at most 0.0049.
Values may be sent and summed in bfloat16 or wider, within the bound.
No kernel may reach another device: no remote copies, remote signals or barrier semaphores. Data moves between devices by JAX's collectives and lax.ppermute only.
A program may use at most 64 MiB of HBM per device.

```python
import math
import jax
import jax.numpy as jnp
from jax import lax

D = 30
FATES = 40
N = 4096
ITERS = 8
PAIRS = 4


def draw_live(key, part):
    first_key, second_key = jax.random.split(key)
    counts = jax.random.randint(first_key, (PAIRS + 1,), N // 4, N + 1)
    filled = jax.random.randint(second_key, (), 0, PAIRS + 1)
    return jnp.where(jnp.arange(PAIRS + 1) == filled, N, counts).astype(jnp.int32)


def atlas_tables(key):
    lineages = 32
    lineage_base = jax.random.uniform(jax.random.fold_in(key, 101), (lineages, D), jnp.float32, -3.0, 3.0)
    section_reach = jnp.exp(jax.random.uniform(jax.random.fold_in(key, 102), (lineages, 1), jnp.float32, math.log(1.5), math.log(4.5)))
    sign_table = jax.random.randint(jax.random.fold_in(key, 103), (lineages, D), 0, 2).astype(jnp.float32) * 2.0 - 1.0
    section_step = section_reach * sign_table / math.sqrt(D)
    centres = jnp.stack([lineage_base, lineage_base + section_step], axis=1).reshape(2 * lineages, D)
    fate_of = (jax.random.permutation(jax.random.fold_in(key, 104), 2 * lineages) % FATES).astype(jnp.int32)
    flip_signs = jax.random.randint(jax.random.fold_in(key, 105), (D,), 0, 2).astype(jnp.float32) * 2.0 - 1.0
    return (centres, fate_of, flip_signs)


def cell_states(key, snapshot):
    lineages = 32
    snap_key = jax.random.fold_in(jax.random.fold_in(key, 201), snapshot)
    lineage = jax.random.randint(jax.random.fold_in(snap_key, 1), (N,), 0, lineages)
    section_share = jax.random.randint(jax.random.fold_in(snap_key, 2), (lineages,), 15, 86)
    section_roll = jax.random.randint(jax.random.fold_in(snap_key, 3), (N,), 0, 100)
    section_bit = (section_roll < section_share[lineage]).astype(jnp.int32)
    return (2 * lineage + section_bit).astype(jnp.int32)


def place_cells(key, snapshot, jitter):
    centres, fate_of, flip_signs = atlas_tables(key)
    states = cell_states(key, snapshot)
    offset_side = 10.0 - 20.0 * (snapshot % 2)
    return offset_side * flip_signs[:, None] + centres[states].T + jitter


def draw_src_cells(key, part):
    jitter_key = jax.random.fold_in(key, 21)
    jitter = jnp.clip(jax.random.normal(jitter_key, (PAIRS, D, N), jnp.float32), -3.0, 3.0)
    return jnp.stack([place_cells(key, snapshot, jitter[snapshot]) for snapshot in range(PAIRS)])


def draw_final_cells(key, part):
    jitter_key = jax.random.fold_in(key, 31)
    jitter = jnp.clip(jax.random.normal(jitter_key, (D, N), jnp.float32), -3.0, 3.0)
    return place_cells(key, PAIRS, jitter)


def draw_final_fates(key, part):
    centres, fate_of, flip_signs = atlas_tables(key)
    states = cell_states(key, PAIRS)
    fate_ids = fate_of[states]
    marked = (jnp.arange(FATES, dtype=jnp.int32)[:, None] == fate_ids[None, :]).astype(jnp.float32)
    background = jax.random.uniform(jax.random.fold_in(key, 301), (FATES, N), jnp.float32, 0.0, 1.0)
    return 0.8 * marked + 0.2 * background


def levels(own_key, dims, cuts, least, high):
    factor_of, own = 1.0, jax.random.fold_in(own_key, 6)
    for position, parts in cuts:
        heights = jnp.exp(jax.random.uniform(jax.random.fold_in(own, position), (parts,), jnp.float32, least / len(cuts), high / len(cuts)))
        factor_of = factor_of * jnp.repeat(heights, dims[position] // parts).reshape([-1 if axis == position else 1 for axis in range(len(dims))])
    return factor_of


def setup_inputs(seed: int = 0) -> dict:
    key_list = jax.random.split(jax.random.key(seed), 6)
    src_cells = draw_src_cells(jax.random.fold_in(key_list[5], 71), 0)
    final_cells = draw_final_cells(jax.random.fold_in(key_list[5], 71), 0)
    growth = jnp.clip(jnp.exp(math.log(2.0) - 1.3862944 * jax.random.uniform(key_list[2], (PAIRS, N), jnp.float32) ** levels(key_list[2], (PAIRS, N), ((0, 4), (1, 2)), -0.2, 0.2)), 0.5, 2.0)
    live = draw_live(jax.random.fold_in(key_list[5], 71), 0)
    final_fates = draw_final_fates(jax.random.fold_in(key_list[5], 71), 0)
    return dict(src_cells=src_cells, final_cells=final_cells, growth=growth, live=live, final_fates=final_fates)


EPS = 0.1
LAM = 1.0
NEG = -1.0e30


def pair_cost(source_pos, target_pos):
    cross = lax.dot_general(source_pos, target_pos, (((0,), (0,)), ((), ())), precision=lax.Precision.HIGHEST, preferred_element_type=jnp.float32)
    src_sq = jnp.sum(source_pos * source_pos, axis=0)
    tgt_sq = jnp.sum(target_pos * target_pos, axis=0)
    return (src_sq[:, None] + tgt_sq[None, :] - 2.0 * cross) / (2.0 * source_pos.shape[0])


def reference(src_cells, final_cells, growth, live, final_fates):
    shrink = LAM / (LAM + EPS)
    pair_count = src_cells.shape[0]
    slots = src_cells.shape[2]
    positions = jnp.arange(slots, dtype=jnp.int32)
    handed = final_fates.astype(jnp.bfloat16)
    fate_list = [None] * pair_count
    pot_list = [None] * pair_count
    for pair_num in reversed(range(pair_count)):
        source_pos = src_cells[pair_num]
        target_pos = src_cells[pair_num + 1] if pair_num + 1 < pair_count else final_cells
        cost_tile = pair_cost(source_pos, target_pos)
        live_src = positions < live[pair_num]
        live_tgt = positions < live[pair_num + 1]
        log_mass_a = jnp.where(live_src, jnp.log(growth[pair_num]) - jnp.log(live[pair_num].astype(jnp.float32)), NEG)
        log_mass_b = jnp.where(live_tgt, -jnp.log(live[pair_num + 1].astype(jnp.float32)) * jnp.ones((slots,), jnp.float32), NEG)
        pot_src = jnp.zeros((slots,), jnp.float32)
        pot_tgt = jnp.zeros((slots,), jnp.float32)
        for step_num in range(ITERS):
            col_scores = (pot_src[:, None] - cost_tile) / EPS + log_mass_a[:, None]
            col_peak = jnp.max(col_scores, axis=0)
            col_total = jnp.sum(jnp.exp(col_scores - col_peak[None, :]), axis=0)
            pot_tgt = -shrink * EPS * (col_peak + jnp.log(col_total))
            row_scores = (pot_tgt[None, :] - cost_tile) / EPS + log_mass_b[None, :]
            row_peak = jnp.max(row_scores, axis=1)
            row_total = jnp.sum(jnp.exp(row_scores - row_peak[:, None]), axis=1)
            pot_src = -shrink * EPS * (row_peak + jnp.log(row_total))
        weights = (jnp.exp(row_scores - row_peak[:, None]) / row_total[:, None]).astype(jnp.bfloat16)
        pulled = lax.dot_general(handed, weights, (((1,), (1,)), ((), ())), preferred_element_type=jnp.float32)
        pulled = jnp.where(live_src[None, :], pulled, 0.0)
        fate_list[pair_num] = pulled
        pot_list[pair_num] = pot_src
        handed = pulled.astype(jnp.bfloat16)
    return jnp.stack(fate_list), jnp.stack(pot_list)
```

```python
import jax
import jax.numpy as jnp
from jax import lax
from jax.sharding import PartitionSpec as P

ITERS = 8


EPS = 0.1
LAM = 1.0
NEG = -1e30


def shifted(shard, axis, by):
    devices = lax.axis_size(axis)
    pairs = [(i, i + by) for i in range(devices) if 0 <= i + by < devices]
    return lax.ppermute(shard, axis, pairs)


def local(src_cells, final_cells, growth, live, final_fates):
    pair_count = lax.axis_size("pair")
    tgt_count = lax.axis_size("tgt")
    pair_rank = lax.axis_index("pair")
    src_rank = lax.axis_index("src")
    tgt_rank = lax.axis_index("tgt")
    shrink = LAM / (LAM + EPS)
    source_all = src_cells[0]
    dims = source_all.shape[0]
    src_width = source_all.shape[1]
    rows = src_width // tgt_count
    row_off = tgt_rank * rows
    is_last = pair_rank == pair_count - 1
    source_pos = lax.dynamic_slice_in_dim(source_all, row_off, rows, 1)
    arrived = lax.all_gather(shifted(source_all, "pair", -1), "src", axis=1, tiled=True)
    final_all = lax.all_gather(final_cells, "tgt", axis=1, tiled=True)
    target_pos = jnp.where(is_last, final_all, arrived)
    cols = target_pos.shape[1]
    cross = lax.dot_general(
        source_pos,
        target_pos,
        (((0,), (0,)), ((), ())),
        precision=lax.Precision.HIGHEST,
        preferred_element_type=jnp.float32,
    )
    src_sq = jnp.sum(source_pos * source_pos, axis=0)
    tgt_sq = jnp.sum(target_pos * target_pos, axis=0)
    cost_tile = (src_sq[:, None] + tgt_sq[None, :] - 2.0 * cross) / (2.0 * dims)
    live_now = lax.dynamic_index_in_dim(live, pair_rank, keepdims=False)
    live_next = lax.dynamic_index_in_dim(live, pair_rank + 1, keepdims=False)
    row_index = src_rank * src_width + row_off + jnp.arange(rows, dtype=jnp.int32)
    col_index = jnp.arange(cols, dtype=jnp.int32)
    live_src = row_index < live_now
    live_tgt = col_index < live_next
    growth_rows = lax.dynamic_slice_in_dim(growth[0], row_off, rows, 0)
    log_mass_a = jnp.where(
        live_src, jnp.log(growth_rows) - jnp.log(live_now.astype(jnp.float32)), NEG
    )
    log_mass_b = jnp.where(
        live_tgt, -jnp.log(live_next.astype(jnp.float32)) * jnp.ones((cols,), jnp.float32), NEG
    )
    pot_src = jnp.zeros((rows,), jnp.float32)
    for step_num in range(ITERS):
        col_scores = (pot_src[:, None] - cost_tile) / EPS + log_mass_a[:, None]
        col_peak = jnp.max(col_scores, axis=0)
        col_total = jnp.sum(jnp.exp(col_scores - col_peak[None, :]), axis=0)
        part_lse = col_peak + jnp.log(col_total)
        every = lax.all_gather(part_lse, ("src", "tgt"))
        every_peak = jnp.max(every, axis=0)
        col_lse = every_peak + jnp.log(jnp.sum(jnp.exp(every - every_peak[None, :]), axis=0))
        pot_tgt = -shrink * EPS * col_lse
        row_scores = (pot_tgt[None, :] - cost_tile) / EPS + log_mass_b[None, :]
        row_peak = jnp.max(row_scores, axis=1)
        row_total = jnp.sum(jnp.exp(row_scores - row_peak[:, None]), axis=1)
        pot_src = -shrink * EPS * (row_peak + jnp.log(row_total))
    weights = (jnp.exp(row_scores - row_peak[:, None]) / row_total[:, None]).astype(jnp.bfloat16)
    final_handed = lax.all_gather(final_fates.astype(jnp.bfloat16), "tgt", axis=1, tiled=True)
    handed = jnp.where(is_last, final_handed, jnp.zeros(final_handed.shape, jnp.bfloat16))
    fate_maps = jnp.zeros((final_fates.shape[0], rows), jnp.float32)
    for section_num in range(pair_count):
        active = pair_count - 1 - section_num
        pulled = lax.dot_general(
            handed, weights, (((1,), (1,)), ((), ())), preferred_element_type=jnp.float32
        )
        pulled = jnp.where(live_src[None, :], pulled, 0.0)
        fate_maps = jnp.where(pair_rank == active, pulled, fate_maps)
        if section_num + 1 < pair_count:
            passed = shifted(pulled.astype(jnp.bfloat16), "pair", -1)
            fresh = lax.all_gather(passed, ("src", "tgt"), axis=1, tiled=True)
            handed = jnp.where(pair_rank == active - 1, fresh, handed)
    pot_all = lax.all_gather(pot_src, "tgt", axis=0, tiled=True)
    return (fate_maps[None], pot_all[None])


def solution(mesh):
    placed = (P("pair", None, "src"), P(None, "tgt"), P("pair", "src"), P(), P(None, "tgt"))
    return jax.shard_map(
        local,
        mesh=mesh,
        in_specs=placed,
        out_specs=(P("pair", None, ("src", "tgt")), P("pair", "src")),
        check_vma=False,
    )
```

```python
import jax
import jax.numpy as jnp
from jax import lax
from jax.sharding import PartitionSpec as P

ITERS = 8


EPS = 0.1
LAM = 1.0
NEG = -1e30


def shifted(shard, axis, by):
    devices = lax.axis_size(axis)
    pairs = [(i, i + by) for i in range(devices) if 0 <= i + by < devices]
    return lax.ppermute(shard, axis, pairs)


def local(src_cells, final_cells, growth, live, final_fates):
    pair_count = lax.axis_size("pair")
    tgt_count = lax.axis_size("tgt")
    pair_rank = lax.axis_index("pair")
    src_rank = lax.axis_index("src")
    tgt_rank = lax.axis_index("tgt")
    shrink = LAM / (LAM + EPS)
    source_all = src_cells[0]
    dims = source_all.shape[0]
    src_width = source_all.shape[1]
    rows = src_width // tgt_count
    row_off = tgt_rank * rows
    is_last = pair_rank == pair_count - 1
    source_pos = lax.dynamic_slice_in_dim(source_all, row_off, rows, 1)
    arrived = lax.all_gather(shifted(source_all, "pair", -1), "src", axis=1, tiled=True)
    final_all = lax.all_gather(final_cells, "tgt", axis=1, tiled=True)
    target_pos = jnp.where(is_last, final_all, arrived)
    cols = target_pos.shape[1]
    cross = lax.dot_general(
        source_pos,
        target_pos,
        (((0,), (0,)), ((), ())),
        precision=lax.Precision.HIGHEST,
        preferred_element_type=jnp.float32,
    )
    src_sq = jnp.sum(source_pos * source_pos, axis=0)
    tgt_sq = jnp.sum(target_pos * target_pos, axis=0)
    cost_tile = (src_sq[:, None] + tgt_sq[None, :] - 2.0 * cross) / (2.0 * dims)
    live_now = lax.dynamic_index_in_dim(live, pair_rank, keepdims=False)
    live_next = lax.dynamic_index_in_dim(live, pair_rank + 1, keepdims=False)
    row_index = src_rank * src_width + row_off + jnp.arange(rows, dtype=jnp.int32)
    col_index = jnp.arange(cols, dtype=jnp.int32)
    live_src = row_index < live_now
    live_tgt = col_index < live_next
    growth_rows = lax.dynamic_slice_in_dim(growth[0], row_off, rows, 0)
    log_mass_a = jnp.where(
        live_src, jnp.log(growth_rows) - jnp.log(live_now.astype(jnp.float32)), NEG
    )
    log_mass_b = jnp.where(
        live_tgt, -jnp.log(live_next.astype(jnp.float32)) * jnp.ones((cols,), jnp.float32), NEG
    )
    scaled_cost = cost_tile * (1.0 / EPS)
    pot_src = jnp.zeros((rows,), jnp.float32)
    for step_num in range(ITERS):
        row_shift = pot_src * (1.0 / EPS) + log_mass_a
        col_scores = row_shift[:, None] - scaled_cost
        col_peak = jnp.max(col_scores, axis=0)
        col_total = jnp.sum(jnp.exp(col_scores - col_peak[None, :]), axis=0)
        part_lse = col_peak + jnp.log(col_total)
        every = lax.all_gather(part_lse, ("src", "tgt"))
        every_peak = jnp.max(every, axis=0)
        col_lse = every_peak + jnp.log(jnp.sum(jnp.exp(every - every_peak[None, :]), axis=0))
        pot_tgt = -shrink * EPS * col_lse
        col_shift = pot_tgt * (1.0 / EPS) + log_mass_b
        row_scores = col_shift[None, :] - scaled_cost
        row_peak = jnp.max(row_scores, axis=1)
        row_total = jnp.sum(jnp.exp(row_scores - row_peak[:, None]), axis=1)
        pot_src = -shrink * EPS * (row_peak + jnp.log(row_total))
    weights = (jnp.exp(row_scores - row_peak[:, None]) / row_total[:, None]).astype(jnp.bfloat16)
    final_handed = lax.all_gather(final_fates.astype(jnp.bfloat16), "tgt", axis=1, tiled=True)
    handed = jnp.where(is_last, final_handed, jnp.zeros(final_handed.shape, jnp.bfloat16))
    fate_maps = jnp.zeros((final_fates.shape[0], rows), jnp.float32)
    for section_num in range(pair_count):
        active = pair_count - 1 - section_num
        pulled = lax.dot_general(
            handed, weights, (((1,), (1,)), ((), ())), preferred_element_type=jnp.float32
        )
        pulled = jnp.where(live_src[None, :], pulled, 0.0)
        fate_maps = jnp.where(pair_rank == active, pulled, fate_maps)
        if section_num + 1 < pair_count:
            passed = shifted(pulled.astype(jnp.bfloat16), "pair", -1)
            fresh = lax.all_gather(passed, ("src", "tgt"), axis=1, tiled=True)
            handed = jnp.where(pair_rank == active - 1, fresh, handed)
    pot_all = lax.all_gather(pot_src, "tgt", axis=0, tiled=True)
    return (fate_maps[None], pot_all[None])


def solution(mesh):
    placed = (P("pair", None, "src"), P(None, "tgt"), P("pair", "src"), P(), P(None, "tgt"))
    return jax.shard_map(
        local,
        mesh=mesh,
        in_specs=placed,
        out_specs=(P("pair", None, ("src", "tgt")), P("pair", "src")),
        check_vma=False,
    )
```

```python
import jax
import jax.numpy as jnp
from jax import lax
from jax.sharding import PartitionSpec as P
import functools
from jax.experimental import pallas as pl
from jax.experimental.pallas import tpu as pltpu

ITERS = 8


EPS = 0.1
LAM = 1.0
NEG = -1e30


GROUP = 16
WIDTH = 512


def sweep_kernel(do_row, do_col, emit_w, shrink, c_ref, b_ref, la_ref, *rest):
    rest = list(rest)
    f_ref = rest.pop(0) if do_row else None
    lse_ref = rest.pop(0) if do_col else None
    w_ref = rest.pop(0) if emit_w else None
    a_ref = rest.pop(0)
    rows, cols = c_ref.shape
    groups = rows // GROUP
    chunks = cols // WIDTH

    if do_row:
        def row_group(r, carry):
            rs = pl.ds(pl.multiple_of(r * GROUP, GROUP), GROUP)
            m = jnp.full((GROUP, WIDTH), -jnp.inf, jnp.float32)
            for j in range(chunks):
                cs = slice(j * WIDTH, (j + 1) * WIDTH)
                m = jnp.maximum(m, b_ref[:, cs] - c_ref[rs, cs])
            peak = jnp.max(m, axis=1, keepdims=True)
            s = jnp.zeros((GROUP, WIDTH), jnp.float32)
            for j in range(chunks):
                cs = slice(j * WIDTH, (j + 1) * WIDTH)
                s = s + jnp.exp(b_ref[:, cs] - c_ref[rs, cs] - peak)
            total = jnp.sum(s, axis=1, keepdims=True)
            pot = -shrink * EPS * (peak + jnp.log(total))
            f_ref[rs, :] = pot
            a_ref[rs, :] = pot * (1.0 / EPS) + la_ref[rs, :]
            if emit_w:
                for j in range(chunks):
                    cs = slice(j * WIDTH, (j + 1) * WIDTH)
                    e = jnp.exp(b_ref[:, cs] - c_ref[rs, cs] - peak)
                    w_ref[rs, cs] = (e / total).astype(w_ref.dtype)
            return carry
        lax.fori_loop(0, groups, row_group, 0)
    else:
        a_ref[...] = la_ref[...]

    if do_col:
        def col_chunk(j, carry):
            cs = pl.ds(pl.multiple_of(j * WIDTH, WIDTH), WIDTH)

            def peak_group(r, m):
                rs = pl.ds(pl.multiple_of(r * GROUP, GROUP), GROUP)
                return jnp.maximum(m, a_ref[rs, :] - c_ref[rs, cs])
            m = lax.fori_loop(0, groups, peak_group,
                              jnp.full((GROUP, WIDTH), -jnp.inf, jnp.float32))
            peak = jnp.max(m, axis=0, keepdims=True)

            def sum_group(r, s):
                rs = pl.ds(pl.multiple_of(r * GROUP, GROUP), GROUP)
                return s + jnp.exp(a_ref[rs, :] - c_ref[rs, cs] - peak)
            s = lax.fori_loop(0, groups, sum_group, jnp.zeros((GROUP, WIDTH), jnp.float32))
            lse_ref[:, cs] = peak + jnp.log(jnp.sum(s, axis=0, keepdims=True))
            return carry
        lax.fori_loop(0, chunks, col_chunk, 0)


def sweep(scaled_cost, col_shift, log_a, shrink, do_row, do_col, emit_w):
    rows, cols = scaled_cost.shape
    outs = []
    if do_row:
        outs.append(jax.ShapeDtypeStruct((rows, 1), jnp.float32))
    if do_col:
        outs.append(jax.ShapeDtypeStruct((1, cols), jnp.float32))
    if emit_w:
        outs.append(jax.ShapeDtypeStruct((rows, cols), jnp.bfloat16))
    passes = (2 if do_row else 0) + (2 if do_col else 0) + (1 if emit_w else 0)
    vmem = pl.BlockSpec(memory_space=pltpu.VMEM)
    return pl.pallas_call(
        functools.partial(sweep_kernel, do_row, do_col, emit_w, shrink),
        out_shape=tuple(outs),
        in_specs=[vmem] * 3,
        out_specs=tuple([vmem] * len(outs)),
        scratch_shapes=[pltpu.VMEM((rows, 1), jnp.float32)],
        compiler_params=pltpu.CompilerParams(vmem_limit_bytes=48 * 1024 * 1024),
        cost_estimate=pl.CostEstimate(
            flops=4 * passes * rows * cols,
            transcendentals=passes * rows * cols // 2,
            bytes_accessed=4 * rows * cols + (2 * rows * cols if emit_w else 0),
        ),
    )(scaled_cost, col_shift[None, :], log_a[:, None])


def shifted(shard, axis, by):
    devices = lax.axis_size(axis)
    pairs = [(i, i + by) for i in range(devices) if 0 <= i + by < devices]
    return lax.ppermute(shard, axis, pairs)


def local(src_cells, final_cells, growth, live, final_fates):
    pair_count = lax.axis_size("pair")
    tgt_count = lax.axis_size("tgt")
    pair_rank = lax.axis_index("pair")
    src_rank = lax.axis_index("src")
    tgt_rank = lax.axis_index("tgt")
    shrink = LAM / (LAM + EPS)
    source_all = src_cells[0]
    dims = source_all.shape[0]
    src_width = source_all.shape[1]
    rows = src_width // tgt_count
    row_off = tgt_rank * rows
    is_last = pair_rank == pair_count - 1
    source_pos = lax.dynamic_slice_in_dim(source_all, row_off, rows, 1)
    arrived = lax.all_gather(shifted(source_all, "pair", -1), "src", axis=1, tiled=True)
    final_all = lax.all_gather(final_cells, "tgt", axis=1, tiled=True)
    target_pos = jnp.where(is_last, final_all, arrived)
    cols = target_pos.shape[1]
    cross = lax.dot_general(
        source_pos,
        target_pos,
        (((0,), (0,)), ((), ())),
        precision=lax.Precision.HIGHEST,
        preferred_element_type=jnp.float32,
    )
    src_sq = jnp.sum(source_pos * source_pos, axis=0)
    tgt_sq = jnp.sum(target_pos * target_pos, axis=0)
    cost_tile = (src_sq[:, None] + tgt_sq[None, :] - 2.0 * cross) / (2.0 * dims)
    live_now = lax.dynamic_index_in_dim(live, pair_rank, keepdims=False)
    live_next = lax.dynamic_index_in_dim(live, pair_rank + 1, keepdims=False)
    row_index = src_rank * src_width + row_off + jnp.arange(rows, dtype=jnp.int32)
    col_index = jnp.arange(cols, dtype=jnp.int32)
    live_src = row_index < live_now
    live_tgt = col_index < live_next
    growth_rows = lax.dynamic_slice_in_dim(growth[0], row_off, rows, 0)
    log_mass_a = jnp.where(
        live_src, jnp.log(growth_rows) - jnp.log(live_now.astype(jnp.float32)), NEG
    )
    log_mass_b = jnp.where(
        live_tgt, -jnp.log(live_next.astype(jnp.float32)) * jnp.ones((cols,), jnp.float32), NEG
    )
    scaled_cost = cost_tile * (1.0 / EPS)
    (part_lse,) = sweep(scaled_cost, log_mass_b, log_mass_a, shrink, False, True, False)
    for step_num in range(ITERS):
        every = lax.all_gather(part_lse[0], ("src", "tgt"))
        every_peak = jnp.max(every, axis=0)
        col_lse = every_peak + jnp.log(jnp.sum(jnp.exp(every - every_peak[None, :]), axis=0))
        pot_tgt = -shrink * EPS * col_lse
        col_shift = pot_tgt * (1.0 / EPS) + log_mass_b
        if step_num + 1 < ITERS:
            pot_col, part_lse = sweep(scaled_cost, col_shift, log_mass_a, shrink, True, True, False)
        else:
            pot_col, weights = sweep(scaled_cost, col_shift, log_mass_a, shrink, True, False, True)
    pot_src = pot_col[:, 0]
    final_handed = lax.all_gather(final_fates.astype(jnp.bfloat16), "tgt", axis=1, tiled=True)
    handed = jnp.where(is_last, final_handed, jnp.zeros(final_handed.shape, jnp.bfloat16))
    fate_maps = jnp.zeros((final_fates.shape[0], rows), jnp.float32)
    for section_num in range(pair_count):
        active = pair_count - 1 - section_num
        pulled = lax.dot_general(
            handed, weights, (((1,), (1,)), ((), ())), preferred_element_type=jnp.float32
        )
        pulled = jnp.where(live_src[None, :], pulled, 0.0)
        fate_maps = jnp.where(pair_rank == active, pulled, fate_maps)
        if section_num + 1 < pair_count:
            passed = shifted(pulled.astype(jnp.bfloat16), "pair", -1)
            fresh = lax.all_gather(passed, ("src", "tgt"), axis=1, tiled=True)
            handed = jnp.where(pair_rank == active - 1, fresh, handed)
    pot_all = lax.all_gather(pot_src, "tgt", axis=0, tiled=True)
    return (fate_maps[None], pot_all[None])


def solution(mesh):
    placed = (P("pair", None, "src"), P(None, "tgt"), P("pair", "src"), P(), P(None, "tgt"))
    return jax.shard_map(
        local,
        mesh=mesh,
        in_specs=placed,
        out_specs=(P("pair", None, ("src", "tgt")), P("pair", "src")),
        check_vma=False,
    )
```

```python
import jax
import jax.numpy as jnp
from jax import lax
from jax.sharding import PartitionSpec as P
import functools
from jax.experimental import pallas as pl
from jax.experimental.pallas import tpu as pltpu

ITERS = 8


EPS = 0.1
LAM = 1.0
NEG = -1e30


GROUP = 16
ROW_GROUP = 32
WIDTH = 512


def sweep_kernel(do_row, do_col, emit_w, shrink, c_ref, b_ref, la_ref, *rest):
    rest = list(rest)
    f_ref = rest.pop(0) if do_row else None
    lse_ref = rest.pop(0) if do_col else None
    w_ref = rest.pop(0) if emit_w else None
    a_ref = rest.pop(0)
    rows, cols = c_ref.shape
    groups = rows // GROUP
    chunks = cols // WIDTH

    if do_row:
        rg = ROW_GROUP if rows % ROW_GROUP == 0 else GROUP

        def row_group(r, carry):
            rs = pl.ds(pl.multiple_of(r * rg, rg), rg)
            m = jnp.full((rg, WIDTH), -jnp.inf, jnp.float32)
            for j in range(chunks):
                cs = slice(j * WIDTH, (j + 1) * WIDTH)
                m = jnp.maximum(m, b_ref[:, cs] - c_ref[rs, cs])
            peak = jnp.max(m, axis=1, keepdims=True)
            s = jnp.zeros((rg, WIDTH), jnp.float32)
            for j in range(chunks):
                cs = slice(j * WIDTH, (j + 1) * WIDTH)
                s = s + jnp.exp(b_ref[:, cs] - c_ref[rs, cs] - peak)
            total = jnp.sum(s, axis=1, keepdims=True)
            pot = -shrink * EPS * (peak + jnp.log(total))
            f_ref[rs, :] = pot
            a_ref[rs, :] = jnp.broadcast_to(pot * (1.0 / EPS) + la_ref[rs, :], (rg, 128))
            if emit_w:
                for j in range(chunks):
                    cs = slice(j * WIDTH, (j + 1) * WIDTH)
                    e = jnp.exp(b_ref[:, cs] - c_ref[rs, cs] - peak)
                    w_ref[rs, cs] = (e / total).astype(w_ref.dtype)
            return carry
        lax.fori_loop(0, rows // rg, row_group, 0)
    else:
        a_ref[...] = jnp.broadcast_to(la_ref[...], a_ref.shape)

    if do_col:
        def col_chunk(j, carry):
            cs = pl.ds(pl.multiple_of(j * WIDTH, WIDTH), WIDTH)
            shifts = [jnp.tile(a_ref[r * GROUP:(r + 1) * GROUP, :], (1, WIDTH // 128))
                      for r in range(groups)]
            m = [jnp.full((GROUP, WIDTH), -jnp.inf, jnp.float32) for _ in range(2)]
            for r in range(groups):
                m[r % 2] = jnp.maximum(m[r % 2], shifts[r] - c_ref[r * GROUP:(r + 1) * GROUP, cs])
            peak = jnp.max(jnp.maximum(m[0], m[1]), axis=0, keepdims=True)
            s = [jnp.zeros((GROUP, WIDTH), jnp.float32) for _ in range(2)]
            for r in range(groups):
                s[r % 2] = s[r % 2] + jnp.exp(shifts[r] - c_ref[r * GROUP:(r + 1) * GROUP, cs] - peak)
            lse_ref[:, cs] = peak + jnp.log(jnp.sum(s[0] + s[1], axis=0, keepdims=True))
            return carry
        lax.fori_loop(0, chunks, col_chunk, 0)


def sweep(scaled_cost, col_shift, log_a, shrink, do_row, do_col, emit_w):
    rows, cols = scaled_cost.shape
    outs = []
    if do_row:
        outs.append(jax.ShapeDtypeStruct((rows, 1), jnp.float32))
    if do_col:
        outs.append(jax.ShapeDtypeStruct((1, cols), jnp.float32))
    if emit_w:
        outs.append(jax.ShapeDtypeStruct((rows, cols), jnp.bfloat16))
    passes = (2 if do_row else 0) + (2 if do_col else 0) + (1 if emit_w else 0)
    vmem = pl.BlockSpec(memory_space=pltpu.VMEM)
    return pl.pallas_call(
        functools.partial(sweep_kernel, do_row, do_col, emit_w, shrink),
        out_shape=tuple(outs),
        in_specs=[vmem] * 3,
        out_specs=tuple([vmem] * len(outs)),
        scratch_shapes=[pltpu.VMEM((rows, 128), jnp.float32)],
        compiler_params=pltpu.CompilerParams(vmem_limit_bytes=24 * 1024 * 1024),
        cost_estimate=pl.CostEstimate(
            flops=4 * passes * rows * cols,
            transcendentals=passes * rows * cols // 2,
            bytes_accessed=4 * rows * cols + (2 * rows * cols if emit_w else 0),
        ),
    )(scaled_cost, col_shift[None, :], log_a[:, None])


def shifted(shard, axis, by):
    devices = lax.axis_size(axis)
    pairs = [(i, i + by) for i in range(devices) if 0 <= i + by < devices]
    return lax.ppermute(shard, axis, pairs)


def local(src_cells, final_cells, growth, live, final_fates):
    pair_count = lax.axis_size("pair")
    tgt_count = lax.axis_size("tgt")
    pair_rank = lax.axis_index("pair")
    src_rank = lax.axis_index("src")
    tgt_rank = lax.axis_index("tgt")
    shrink = LAM / (LAM + EPS)
    source_all = src_cells[0]
    dims = source_all.shape[0]
    src_width = source_all.shape[1]
    rows = src_width // tgt_count
    row_off = tgt_rank * rows
    is_last = pair_rank == pair_count - 1
    source_pos = lax.dynamic_slice_in_dim(source_all, row_off, rows, 1)
    arrived = lax.all_gather(shifted(source_all, "pair", -1), "src", axis=1, tiled=True)
    final_all = lax.all_gather(final_cells, "tgt", axis=1, tiled=True)
    target_pos = jnp.where(is_last, final_all, arrived)
    cols = target_pos.shape[1]
    cross = lax.dot_general(
        source_pos,
        target_pos,
        (((0,), (0,)), ((), ())),
        precision=lax.Precision.HIGHEST,
        preferred_element_type=jnp.float32,
    )
    src_sq = jnp.sum(source_pos * source_pos, axis=0)
    tgt_sq = jnp.sum(target_pos * target_pos, axis=0)
    cost_tile = (src_sq[:, None] + tgt_sq[None, :] - 2.0 * cross) / (2.0 * dims)
    live_now = lax.dynamic_index_in_dim(live, pair_rank, keepdims=False)
    live_next = lax.dynamic_index_in_dim(live, pair_rank + 1, keepdims=False)
    row_index = src_rank * src_width + row_off + jnp.arange(rows, dtype=jnp.int32)
    col_index = jnp.arange(cols, dtype=jnp.int32)
    live_src = row_index < live_now
    live_tgt = col_index < live_next
    growth_rows = lax.dynamic_slice_in_dim(growth[0], row_off, rows, 0)
    log_mass_a = jnp.where(
        live_src, jnp.log(growth_rows) - jnp.log(live_now.astype(jnp.float32)), NEG
    )
    log_mass_b = jnp.where(
        live_tgt, -jnp.log(live_next.astype(jnp.float32)) * jnp.ones((cols,), jnp.float32), NEG
    )
    scaled_cost = cost_tile * (1.0 / EPS)
    (part_lse,) = sweep(scaled_cost, log_mass_b, log_mass_a, shrink, False, True, False)
    for step_num in range(ITERS):
        every = lax.all_gather(part_lse[0], ("src", "tgt"))
        every_peak = jnp.max(every, axis=0)
        col_lse = every_peak + jnp.log(jnp.sum(jnp.exp(every - every_peak[None, :]), axis=0))
        pot_tgt = -shrink * EPS * col_lse
        col_shift = pot_tgt * (1.0 / EPS) + log_mass_b
        if step_num + 1 < ITERS:
            pot_col, part_lse = sweep(scaled_cost, col_shift, log_mass_a, shrink, True, True, False)
        else:
            pot_col, weights = sweep(scaled_cost, col_shift, log_mass_a, shrink, True, False, True)
    pot_src = pot_col[:, 0]
    final_handed = lax.all_gather(final_fates.astype(jnp.bfloat16), "tgt", axis=1, tiled=True)
    handed = jnp.where(is_last, final_handed, jnp.zeros(final_handed.shape, jnp.bfloat16))
    fate_maps = jnp.zeros((final_fates.shape[0], rows), jnp.float32)
    for section_num in range(pair_count):
        active = pair_count - 1 - section_num
        pulled = lax.dot_general(
            handed, weights, (((1,), (1,)), ((), ())), preferred_element_type=jnp.float32
        )
        pulled = jnp.where(live_src[None, :], pulled, 0.0)
        fate_maps = jnp.where(pair_rank == active, pulled, fate_maps)
        if section_num + 1 < pair_count:
            passed = shifted(pulled.astype(jnp.bfloat16), "pair", -1)
            fresh = lax.all_gather(passed, ("src", "tgt"), axis=1, tiled=True)
            handed = jnp.where(pair_rank == active - 1, fresh, handed)
    pot_all = lax.all_gather(pot_src, "tgt", axis=0, tiled=True)
    return (fate_maps[None], pot_all[None])


def solution(mesh):
    placed = (P("pair", None, "src"), P(None, "tgt"), P("pair", "src"), P(), P(None, "tgt"))
    return jax.shard_map(
        local,
        mesh=mesh,
        in_specs=placed,
        out_specs=(P("pair", None, ("src", "tgt")), P("pair", "src")),
        check_vma=False,
    )
```

```python
import jax
import jax.numpy as jnp
from jax import lax
from jax.sharding import PartitionSpec as P
import functools
from jax.experimental import pallas as pl
from jax.experimental.pallas import tpu as pltpu

ITERS = 8


EPS = 0.1
LAM = 1.0
NEG = -1e30


GROUP = 16
ROW_GROUP = 32
WIDTH = 512


def sweep_kernel(do_row, do_col, emit_w, shrink, c_ref, b_ref, la_ref, *rest):
    rest = list(rest)
    f_ref = rest.pop(0) if do_row else None
    lse_ref = rest.pop(0) if do_col else None
    w_ref = rest.pop(0) if emit_w else None
    a_ref = rest.pop(0)
    rows, cols = c_ref.shape
    groups = rows // GROUP
    chunks = cols // WIDTH

    if do_row:
        rg = ROW_GROUP if rows % ROW_GROUP == 0 else GROUP

        def row_group(r, carry):
            rs = pl.ds(pl.multiple_of(r * rg, rg), rg)
            m = jnp.full((rg, WIDTH), -jnp.inf, jnp.float32)
            for j in range(chunks):
                cs = slice(j * WIDTH, (j + 1) * WIDTH)
                m = jnp.maximum(m, b_ref[:, cs] - c_ref[rs, cs])
            peak = jnp.max(m, axis=1, keepdims=True)
            s = jnp.zeros((rg, WIDTH), jnp.float32)
            for j in range(chunks):
                cs = slice(j * WIDTH, (j + 1) * WIDTH)
                s = s + jnp.exp(b_ref[:, cs] - c_ref[rs, cs] - peak)
            total = jnp.sum(s, axis=1, keepdims=True)
            pot = -shrink * EPS * (peak + jnp.log(total))
            f_ref[rs, :] = pot
            a_ref[rs, :] = jnp.broadcast_to(pot * (1.0 / EPS) + la_ref[rs, :], (rg, 128))
            if emit_w:
                for j in range(chunks):
                    cs = slice(j * WIDTH, (j + 1) * WIDTH)
                    e = jnp.exp(b_ref[:, cs] - c_ref[rs, cs] - peak)
                    w_ref[rs, cs] = (e / total).astype(w_ref.dtype)
            return carry
        lax.fori_loop(0, rows // rg, row_group, 0)
    else:
        a_ref[...] = jnp.broadcast_to(la_ref[...], a_ref.shape)

    if do_col:
        def col_chunk(j, carry):
            cs = pl.ds(pl.multiple_of(j * WIDTH, WIDTH), WIDTH)
            shifts = [jnp.tile(a_ref[r * GROUP:(r + 1) * GROUP, :], (1, WIDTH // 128))
                      for r in range(groups)]
            m = [jnp.full((GROUP, WIDTH), -jnp.inf, jnp.float32) for _ in range(2)]
            for r in range(groups):
                m[r % 2] = jnp.maximum(m[r % 2], shifts[r] - c_ref[r * GROUP:(r + 1) * GROUP, cs])
            peak = jnp.max(jnp.maximum(m[0], m[1]), axis=0, keepdims=True)
            s = [jnp.zeros((GROUP, WIDTH), jnp.float32) for _ in range(2)]
            for r in range(groups):
                s[r % 2] = s[r % 2] + jnp.exp(shifts[r] - c_ref[r * GROUP:(r + 1) * GROUP, cs] - peak)
            lse_ref[:, cs] = peak + jnp.log(jnp.sum(s[0] + s[1], axis=0, keepdims=True))
            return carry
        lax.fori_loop(0, chunks, col_chunk, 0)


def sweep(scaled_cost, col_shift, log_a, shrink, do_row, do_col, emit_w):
    rows, cols = scaled_cost.shape
    outs = []
    if do_row:
        outs.append(jax.ShapeDtypeStruct((rows, 1), jnp.float32))
    if do_col:
        outs.append(jax.ShapeDtypeStruct((1, cols), jnp.float32))
    if emit_w:
        outs.append(jax.ShapeDtypeStruct((rows, cols), jnp.bfloat16))
    passes = (2 if do_row else 0) + (2 if do_col else 0) + (1 if emit_w else 0)
    vmem = pl.BlockSpec(memory_space=pltpu.VMEM)
    return pl.pallas_call(
        functools.partial(sweep_kernel, do_row, do_col, emit_w, shrink),
        out_shape=tuple(outs),
        in_specs=[vmem] * 3,
        out_specs=tuple([vmem] * len(outs)),
        scratch_shapes=[pltpu.VMEM((rows, 128), jnp.float32)],
        compiler_params=pltpu.CompilerParams(vmem_limit_bytes=24 * 1024 * 1024),
        cost_estimate=pl.CostEstimate(
            flops=4 * passes * rows * cols,
            transcendentals=passes * rows * cols // 2,
            bytes_accessed=4 * rows * cols + (2 * rows * cols if emit_w else 0),
        ),
    )(scaled_cost, col_shift[None, :], log_a[:, None])


def shifted(shard, axis, by):
    devices = lax.axis_size(axis)
    pairs = [(i, i + by) for i in range(devices) if 0 <= i + by < devices]
    return lax.ppermute(shard, axis, pairs)


def blocks_from_group(block, axes, group, lead=None):
    lead_count = 1 if lead is None else lax.axis_size(lead)
    names = axes if lead is None else (lead,) + tuple(axes)
    received = []
    for k in range(group):
        if lead is None and k == 0:
            received.append(block)
            continue
        pairs = []
        for up in range(lead_count):
            down = up if lead is None else up - 1
            if down < 0:
                continue
            for member in range(group):
                pairs.append((up * group + member, down * group + (member + k) % group))
        received.append(lax.ppermute(block, names, pairs))
    return received


def local(src_cells, final_cells, growth, live, final_fates):
    pair_count = lax.axis_size("pair")
    tgt_count = lax.axis_size("tgt")
    pair_rank = lax.axis_index("pair")
    src_rank = lax.axis_index("src")
    tgt_rank = lax.axis_index("tgt")
    group = lax.axis_size("src") * tgt_count
    member_rank = src_rank * tgt_count + tgt_rank
    shrink = LAM / (LAM + EPS)
    source_all = src_cells[0]
    dims = source_all.shape[0]
    src_width = source_all.shape[1]
    rows = src_width // tgt_count
    row_off = tgt_rank * rows
    is_last = pair_rank == pair_count - 1
    source_pos = lax.dynamic_slice_in_dim(source_all, row_off, rows, 1)
    arrived = lax.all_gather(shifted(source_all, "pair", -1), "src", axis=1, tiled=True)
    final_all = lax.all_gather(final_cells, "tgt", axis=1, tiled=True)
    target_pos = jnp.where(is_last, final_all, arrived)
    cols = target_pos.shape[1]
    cross = lax.dot_general(
        source_pos,
        target_pos,
        (((0,), (0,)), ((), ())),
        precision=lax.Precision.HIGHEST,
        preferred_element_type=jnp.float32,
    )
    src_sq = jnp.sum(source_pos * source_pos, axis=0)
    tgt_sq = jnp.sum(target_pos * target_pos, axis=0)
    cost_tile = (src_sq[:, None] + tgt_sq[None, :] - 2.0 * cross) / (2.0 * dims)
    live_now = lax.dynamic_index_in_dim(live, pair_rank, keepdims=False)
    live_next = lax.dynamic_index_in_dim(live, pair_rank + 1, keepdims=False)
    row_index = src_rank * src_width + row_off + jnp.arange(rows, dtype=jnp.int32)
    col_index = jnp.arange(cols, dtype=jnp.int32)
    live_src = row_index < live_now
    live_tgt = col_index < live_next
    growth_rows = lax.dynamic_slice_in_dim(growth[0], row_off, rows, 0)
    log_mass_a = jnp.where(
        live_src, jnp.log(growth_rows) - jnp.log(live_now.astype(jnp.float32)), NEG
    )
    log_mass_b = jnp.where(
        live_tgt, -jnp.log(live_next.astype(jnp.float32)) * jnp.ones((cols,), jnp.float32), NEG
    )
    scaled_cost = cost_tile * (1.0 / EPS)
    (part_lse,) = sweep(scaled_cost, log_mass_b, log_mass_a, shrink, False, True, False)
    for step_num in range(ITERS):
        every = lax.all_gather(part_lse[0], ("src", "tgt"))
        every_peak = jnp.max(every, axis=0)
        col_lse = every_peak + jnp.log(jnp.sum(jnp.exp(every - every_peak[None, :]), axis=0))
        pot_tgt = -shrink * EPS * col_lse
        col_shift = pot_tgt * (1.0 / EPS) + log_mass_b
        if step_num + 1 < ITERS:
            pot_col, part_lse = sweep(scaled_cost, col_shift, log_mass_a, shrink, True, True, False)
        else:
            pot_col, weights = sweep(scaled_cost, col_shift, log_mass_a, shrink, True, False, True)
    pot_src = pot_col[:, 0]
    final_handed = lax.all_gather(final_fates.astype(jnp.bfloat16), "tgt", axis=1, tiled=True)
    handed = jnp.where(is_last, final_handed, jnp.zeros(final_handed.shape, jnp.bfloat16))
    fate_maps = jnp.zeros((final_fates.shape[0], rows), jnp.float32)
    for section_num in range(pair_count):
        active = pair_count - 1 - section_num
        pulled = lax.dot_general(
            handed, weights, (((1,), (1,)), ((), ())), preferred_element_type=jnp.float32
        )
        pulled = jnp.where(live_src[None, :], pulled, 0.0)
        fate_maps = jnp.where(pair_rank == active, pulled, fate_maps)
        if section_num + 1 < pair_count:
            passed = pulled.astype(jnp.bfloat16)
            if group <= 8:
                got = jnp.stack(blocks_from_group(passed, ("src", "tgt"), group, lead="pair"))
                order = (member_rank - jnp.arange(group, dtype=jnp.int32)) % group
                got = jnp.take(got, order, axis=0)
                fresh = jnp.transpose(got, (1, 0, 2)).reshape(passed.shape[0], group * rows)
            else:
                fresh = lax.all_gather(shifted(passed, "pair", -1), ("src", "tgt"), axis=1, tiled=True)
            handed = jnp.where(pair_rank == active - 1, fresh, handed)
    pot_all = lax.all_gather(pot_src, "tgt", axis=0, tiled=True)
    return (fate_maps[None], pot_all[None])


def solution(mesh):
    placed = (P("pair", None, "src"), P(None, "tgt"), P("pair", "src"), P(), P(None, "tgt"))
    return jax.shard_map(
        local,
        mesh=mesh,
        in_specs=placed,
        out_specs=(P("pair", None, ("src", "tgt")), P("pair", "src")),
        check_vma=False,
    )
```

```python
import jax
import jax.numpy as jnp
from jax import lax
from jax.sharding import PartitionSpec as P
import functools
from jax.experimental import pallas as pl
from jax.experimental.pallas import tpu as pltpu

ITERS = 8


EPS = 0.1
LAM = 1.0
NEG = -1e30


GROUP = 16
ROW_GROUP = 32
WIDTH = 512


def sweep_kernel(do_row, do_col, emit_w, shrink, c_ref, b_ref, la_ref, *rest):
    rest = list(rest)
    f_ref = rest.pop(0) if do_row else None
    lse_ref = rest.pop(0) if do_col else None
    w_ref = rest.pop(0) if emit_w else None
    a_ref = rest.pop(0)
    rows, cols = c_ref.shape
    groups = rows // GROUP
    chunks = cols // WIDTH

    if do_row:
        rg = ROW_GROUP if rows % ROW_GROUP == 0 else GROUP

        def row_group(r, carry):
            rs = pl.ds(pl.multiple_of(r * rg, rg), rg)
            m = jnp.full((rg, WIDTH), -jnp.inf, jnp.float32)
            for j in range(chunks):
                cs = slice(j * WIDTH, (j + 1) * WIDTH)
                m = jnp.maximum(m, b_ref[:, cs] - c_ref[rs, cs])
            peak = jnp.max(m, axis=1, keepdims=True)
            s = jnp.zeros((rg, WIDTH), jnp.float32)
            for j in range(chunks):
                cs = slice(j * WIDTH, (j + 1) * WIDTH)
                s = s + jnp.exp(b_ref[:, cs] - c_ref[rs, cs] - peak)
            total = jnp.sum(s, axis=1, keepdims=True)
            pot = -shrink * EPS * (peak + jnp.log(total))
            f_ref[rs, :] = pot
            a_ref[rs, :] = jnp.broadcast_to(pot * (1.0 / EPS) + la_ref[rs, :], (rg, 128))
            if emit_w:
                for j in range(chunks):
                    cs = slice(j * WIDTH, (j + 1) * WIDTH)
                    e = jnp.exp(b_ref[:, cs] - c_ref[rs, cs] - peak)
                    w_ref[rs, cs] = (e / total).astype(w_ref.dtype)
            return carry
        lax.fori_loop(0, rows // rg, row_group, 0)
    else:
        a_ref[...] = jnp.broadcast_to(la_ref[...], a_ref.shape)

    if do_col:
        def col_chunk(j, carry):
            cs = pl.ds(pl.multiple_of(j * WIDTH, WIDTH), WIDTH)
            shifts = [jnp.tile(a_ref[r * GROUP:(r + 1) * GROUP, :], (1, WIDTH // 128))
                      for r in range(groups)]
            m = [jnp.full((GROUP, WIDTH), -jnp.inf, jnp.float32) for _ in range(2)]
            for r in range(groups):
                m[r % 2] = jnp.maximum(m[r % 2], shifts[r] - c_ref[r * GROUP:(r + 1) * GROUP, cs])
            peak = jnp.max(jnp.maximum(m[0], m[1]), axis=0, keepdims=True)
            s = [jnp.zeros((GROUP, WIDTH), jnp.float32) for _ in range(2)]
            for r in range(groups):
                s[r % 2] = s[r % 2] + jnp.exp(shifts[r] - c_ref[r * GROUP:(r + 1) * GROUP, cs] - peak)
            lse_ref[:, cs] = peak + jnp.log(jnp.sum(s[0] + s[1], axis=0, keepdims=True))
            return carry
        lax.fori_loop(0, chunks, col_chunk, 0)


def sweep(scaled_cost, col_shift, log_a, shrink, do_row, do_col, emit_w):
    rows, cols = scaled_cost.shape
    outs = []
    if do_row:
        outs.append(jax.ShapeDtypeStruct((rows, 1), jnp.float32))
    if do_col:
        outs.append(jax.ShapeDtypeStruct((1, cols), jnp.float32))
    if emit_w:
        outs.append(jax.ShapeDtypeStruct((rows, cols), jnp.bfloat16))
    passes = (2 if do_row else 0) + (2 if do_col else 0) + (1 if emit_w else 0)
    vmem = pl.BlockSpec(memory_space=pltpu.VMEM)
    return pl.pallas_call(
        functools.partial(sweep_kernel, do_row, do_col, emit_w, shrink),
        out_shape=tuple(outs),
        in_specs=[vmem] * 3,
        out_specs=tuple([vmem] * len(outs)),
        scratch_shapes=[pltpu.VMEM((rows, 128), jnp.float32)],
        compiler_params=pltpu.CompilerParams(vmem_limit_bytes=24 * 1024 * 1024),
        cost_estimate=pl.CostEstimate(
            flops=4 * passes * rows * cols,
            transcendentals=passes * rows * cols // 2,
            bytes_accessed=4 * rows * cols + (2 * rows * cols if emit_w else 0),
        ),
    )(scaled_cost, col_shift[None, :], log_a[:, None])


def shifted(shard, axis, by):
    devices = lax.axis_size(axis)
    pairs = [(i, i + by) for i in range(devices) if 0 <= i + by < devices]
    return lax.ppermute(shard, axis, pairs)


def local(src_cells, final_cells, growth, live, final_fates):
    pair_count = lax.axis_size("pair")
    tgt_count = lax.axis_size("tgt")
    pair_rank = lax.axis_index("pair")
    src_rank = lax.axis_index("src")
    tgt_rank = lax.axis_index("tgt")
    shrink = LAM / (LAM + EPS)
    source_all = src_cells[0]
    dims = source_all.shape[0]
    src_width = source_all.shape[1]
    rows = src_width // tgt_count
    row_off = tgt_rank * rows
    is_last = pair_rank == pair_count - 1
    source_pos = lax.dynamic_slice_in_dim(source_all, row_off, rows, 1)
    group = lax.axis_size("src") * tgt_count
    src_count = lax.axis_size("src")
    arrived = shifted(source_all, "pair", -1)
    mine_next = lax.dynamic_slice_in_dim(arrived, row_off, rows, 1)
    fin_width = final_cells.shape[1]
    mine_final = lax.dynamic_slice_in_dim(final_cells, (src_rank * rows) % fin_width, rows, 1)
    piece = jnp.where(is_last, mine_final, mine_next)
    pieces = lax.all_gather(piece, ("src", "tgt"))
    per_fin = fin_width // rows
    final_order = [
        (b % per_fin) * tgt_count + b // per_fin if per_fin == src_count else b for b in range(group)
    ]
    if per_fin == src_count:
        final_pieces = pieces[jnp.array(final_order, dtype=jnp.int32)]
        pieces = jnp.where(is_last, final_pieces, pieces)
        target_pos = jnp.transpose(pieces, (1, 0, 2)).reshape(dims, group * rows)
    else:
        final_all = lax.all_gather(final_cells, "tgt", axis=1, tiled=True)
        target_pos = jnp.where(
            is_last, final_all, jnp.transpose(pieces, (1, 0, 2)).reshape(dims, group * rows)
        )
    cols = target_pos.shape[1]
    cross = lax.dot_general(
        source_pos,
        target_pos,
        (((0,), (0,)), ((), ())),
        precision=lax.Precision.HIGHEST,
        preferred_element_type=jnp.float32,
    )
    src_sq = jnp.sum(source_pos * source_pos, axis=0)
    tgt_sq = jnp.sum(target_pos * target_pos, axis=0)
    cost_tile = (src_sq[:, None] + tgt_sq[None, :] - 2.0 * cross) / (2.0 * dims)
    live_now = lax.dynamic_index_in_dim(live, pair_rank, keepdims=False)
    live_next = lax.dynamic_index_in_dim(live, pair_rank + 1, keepdims=False)
    row_index = src_rank * src_width + row_off + jnp.arange(rows, dtype=jnp.int32)
    col_index = jnp.arange(cols, dtype=jnp.int32)
    live_src = row_index < live_now
    live_tgt = col_index < live_next
    growth_rows = lax.dynamic_slice_in_dim(growth[0], row_off, rows, 0)
    log_mass_a = jnp.where(
        live_src, jnp.log(growth_rows) - jnp.log(live_now.astype(jnp.float32)), NEG
    )
    log_mass_b = jnp.where(
        live_tgt, -jnp.log(live_next.astype(jnp.float32)) * jnp.ones((cols,), jnp.float32), NEG
    )
    scaled_cost = cost_tile * (1.0 / EPS)
    (part_lse,) = sweep(scaled_cost, log_mass_b, log_mass_a, shrink, False, True, False)
    for step_num in range(ITERS):
        every = lax.all_gather(part_lse[0], ("src", "tgt"))
        every_peak = jnp.max(every, axis=0)
        col_lse = every_peak + jnp.log(jnp.sum(jnp.exp(every - every_peak[None, :]), axis=0))
        pot_tgt = -shrink * EPS * col_lse
        col_shift = pot_tgt * (1.0 / EPS) + log_mass_b
        if step_num + 1 < ITERS:
            pot_col, part_lse = sweep(scaled_cost, col_shift, log_mass_a, shrink, True, True, False)
        else:
            pot_col, weights = sweep(scaled_cost, col_shift, log_mass_a, shrink, True, False, True)
    pot_src = pot_col.reshape(rows)
    final_handed = lax.all_gather(final_fates.astype(jnp.bfloat16), "tgt", axis=1, tiled=True)
    handed = jnp.where(is_last, final_handed, jnp.zeros(final_handed.shape, jnp.bfloat16))
    fate_maps = jnp.zeros((final_fates.shape[0], rows), jnp.float32)
    for section_num in range(pair_count):
        active = pair_count - 1 - section_num
        pulled = lax.dot_general(
            handed, weights, (((1,), (1,)), ((), ())), preferred_element_type=jnp.float32
        )
        pulled = jnp.where(live_src[None, :], pulled, 0.0)
        fate_maps = jnp.where(pair_rank == active, pulled, fate_maps)
        if section_num + 1 < pair_count:
            passed = shifted(pulled.astype(jnp.bfloat16), "pair", -1)
            fresh = lax.all_gather(passed, ("src", "tgt"), axis=1, tiled=True)
            handed = jnp.where(pair_rank == active - 1, fresh, handed)
    pot_all = lax.all_gather(pot_src, "tgt", axis=0, tiled=True)
    return (fate_maps[None], pot_all[None])


def solution(mesh):
    placed = (P("pair", None, "src"), P(None, "tgt"), P("pair", "src"), P(), P(None, "tgt"))
    return jax.shard_map(
        local,
        mesh=mesh,
        in_specs=placed,
        out_specs=(P("pair", None, ("src", "tgt")), P("pair", "src")),
        check_vma=False,
    )
```

```python
import jax
import jax.numpy as jnp
from jax import lax
from jax.sharding import PartitionSpec as P
import functools
from jax.experimental import pallas as pl
from jax.experimental.pallas import tpu as pltpu

ITERS = 8


EPS = 0.1
LAM = 1.0
NEG = -1e30


GROUP = 16
ROW_GROUP = 32
WIDTH = 512


def sweep_kernel(do_row, do_col, emit_w, shrink, c_ref, b_ref, la_ref, *rest):
    rest = list(rest)
    f_ref = rest.pop(0) if do_row else None
    lse_ref = rest.pop(0) if do_col else None
    w_ref = rest.pop(0) if emit_w else None
    a_ref = rest.pop(0)
    rows, cols = c_ref.shape
    groups = rows // GROUP
    chunks = cols // WIDTH

    if do_row:
        rg = ROW_GROUP if rows % ROW_GROUP == 0 else GROUP

        def row_group(r, carry):
            rs = pl.ds(pl.multiple_of(r * rg, rg), rg)
            m = jnp.full((rg, WIDTH), -jnp.inf, jnp.float32)
            for j in range(chunks):
                cs = slice(j * WIDTH, (j + 1) * WIDTH)
                m = jnp.maximum(m, b_ref[:, cs] - c_ref[rs, cs])
            peak = jnp.max(m, axis=1, keepdims=True)
            s = jnp.zeros((rg, WIDTH), jnp.float32)
            for j in range(chunks):
                cs = slice(j * WIDTH, (j + 1) * WIDTH)
                s = s + jnp.exp(b_ref[:, cs] - c_ref[rs, cs] - peak)
            total = jnp.sum(s, axis=1, keepdims=True)
            pot = -shrink * EPS * (peak + jnp.log(total))
            f_ref[rs, :] = pot
            a_ref[rs, :] = jnp.broadcast_to(pot * (1.0 / EPS) + la_ref[rs, :], (rg, 128))
            if emit_w:
                for j in range(chunks):
                    cs = slice(j * WIDTH, (j + 1) * WIDTH)
                    e = jnp.exp(b_ref[:, cs] - c_ref[rs, cs] - peak)
                    w_ref[rs, cs] = (e / total).astype(w_ref.dtype)
            return carry
        lax.fori_loop(0, rows // rg, row_group, 0)
    else:
        a_ref[...] = jnp.broadcast_to(la_ref[...], a_ref.shape)

    if do_col:
        def col_chunk(j, carry):
            cs = pl.ds(pl.multiple_of(j * WIDTH, WIDTH), WIDTH)
            shifts = [jnp.tile(a_ref[r * GROUP:(r + 1) * GROUP, :], (1, WIDTH // 128))
                      for r in range(groups)]
            m = [jnp.full((GROUP, WIDTH), -jnp.inf, jnp.float32) for _ in range(2)]
            for r in range(groups):
                m[r % 2] = jnp.maximum(m[r % 2], shifts[r] - c_ref[r * GROUP:(r + 1) * GROUP, cs])
            peak = jnp.max(jnp.maximum(m[0], m[1]), axis=0, keepdims=True)
            s = [jnp.zeros((GROUP, WIDTH), jnp.float32) for _ in range(2)]
            for r in range(groups):
                s[r % 2] = s[r % 2] + jnp.exp(shifts[r] - c_ref[r * GROUP:(r + 1) * GROUP, cs] - peak)
            lse_ref[:, cs] = peak + jnp.log(jnp.sum(s[0] + s[1], axis=0, keepdims=True))
            return carry
        lax.fori_loop(0, chunks, col_chunk, 0)


def sweep(scaled_cost, col_shift, log_a, shrink, do_row, do_col, emit_w):
    rows, cols = scaled_cost.shape
    outs = []
    if do_row:
        outs.append(jax.ShapeDtypeStruct((rows, 1), jnp.float32))
    if do_col:
        outs.append(jax.ShapeDtypeStruct((1, cols), jnp.float32))
    if emit_w:
        outs.append(jax.ShapeDtypeStruct((rows, cols), jnp.bfloat16))
    passes = (2 if do_row else 0) + (2 if do_col else 0) + (1 if emit_w else 0)
    vmem = pl.BlockSpec(memory_space=pltpu.VMEM)
    return pl.pallas_call(
        functools.partial(sweep_kernel, do_row, do_col, emit_w, shrink),
        out_shape=tuple(outs),
        in_specs=[vmem] * 3,
        out_specs=tuple([vmem] * len(outs)),
        scratch_shapes=[pltpu.VMEM((rows, 128), jnp.float32)],
        compiler_params=pltpu.CompilerParams(vmem_limit_bytes=24 * 1024 * 1024),
        cost_estimate=pl.CostEstimate(
            flops=4 * passes * rows * cols,
            transcendentals=passes * rows * cols // 2,
            bytes_accessed=4 * rows * cols + (2 * rows * cols if emit_w else 0),
        ),
    )(scaled_cost, col_shift[None, :], log_a[:, None])


def shifted(shard, axis, by):
    devices = lax.axis_size(axis)
    pairs = [(i, i + by) for i in range(devices) if 0 <= i + by < devices]
    return lax.ppermute(shard, axis, pairs)


def local(src_cells, final_cells, growth, live, final_fates):
    pair_count = lax.axis_size("pair")
    tgt_count = lax.axis_size("tgt")
    pair_rank = lax.axis_index("pair")
    src_rank = lax.axis_index("src")
    tgt_rank = lax.axis_index("tgt")
    shrink = LAM / (LAM + EPS)
    source_all = src_cells[0]
    dims = source_all.shape[0]
    src_width = source_all.shape[1]
    rows = src_width // tgt_count
    row_off = tgt_rank * rows
    is_last = pair_rank == pair_count - 1
    source_pos = lax.dynamic_slice_in_dim(source_all, row_off, rows, 1)
    group = lax.axis_size("src") * tgt_count
    src_count = lax.axis_size("src")
    arrived = shifted(source_all, "pair", -1)
    mine_next = lax.dynamic_slice_in_dim(arrived, row_off, rows, 1)
    fin_width = final_cells.shape[1]
    mine_final = lax.dynamic_slice_in_dim(final_cells, (src_rank * rows) % fin_width, rows, 1)
    piece = jnp.where(is_last, mine_final, mine_next)
    pieces = lax.all_gather(piece, ("src", "tgt"))
    per_fin = fin_width // rows
    final_order = [
        (b % per_fin) * tgt_count + b // per_fin if per_fin == src_count else b for b in range(group)
    ]
    if per_fin == src_count:
        final_pieces = pieces[jnp.array(final_order, dtype=jnp.int32)]
        pieces = jnp.where(is_last, final_pieces, pieces)
        target_pos = jnp.transpose(pieces, (1, 0, 2)).reshape(dims, group * rows)
    else:
        final_all = lax.all_gather(final_cells, "tgt", axis=1, tiled=True)
        target_pos = jnp.where(
            is_last, final_all, jnp.transpose(pieces, (1, 0, 2)).reshape(dims, group * rows)
        )
    cols = target_pos.shape[1]
    cross = lax.dot_general(
        source_pos,
        target_pos,
        (((0,), (0,)), ((), ())),
        precision=lax.Precision.HIGHEST,
        preferred_element_type=jnp.float32,
    )
    src_sq = jnp.sum(source_pos * source_pos, axis=0)
    tgt_sq = jnp.sum(target_pos * target_pos, axis=0)
    cost_tile = (src_sq[:, None] + tgt_sq[None, :] - 2.0 * cross) / (2.0 * dims)
    live_now = lax.dynamic_index_in_dim(live, pair_rank, keepdims=False)
    live_next = lax.dynamic_index_in_dim(live, pair_rank + 1, keepdims=False)
    row_index = src_rank * src_width + row_off + jnp.arange(rows, dtype=jnp.int32)
    col_index = jnp.arange(cols, dtype=jnp.int32)
    live_src = row_index < live_now
    live_tgt = col_index < live_next
    growth_rows = lax.dynamic_slice_in_dim(growth[0], row_off, rows, 0)
    log_mass_a = jnp.where(
        live_src, jnp.log(growth_rows) - jnp.log(live_now.astype(jnp.float32)), NEG
    )
    log_mass_b = jnp.where(
        live_tgt, -jnp.log(live_next.astype(jnp.float32)) * jnp.ones((cols,), jnp.float32), NEG
    )
    scaled_cost = cost_tile * (1.0 / EPS)
    (part_lse,) = sweep(scaled_cost, log_mass_b, log_mass_a, shrink, False, True, False)
    for step_num in range(ITERS):
        every = lax.all_gather(part_lse[0], ("src", "tgt"))
        every_peak = jnp.max(every, axis=0)
        col_lse = every_peak + jnp.log(jnp.sum(jnp.exp(every - every_peak[None, :]), axis=0))
        pot_tgt = -shrink * EPS * col_lse
        col_shift = pot_tgt * (1.0 / EPS) + log_mass_b
        if step_num + 1 < ITERS:
            pot_col, part_lse = sweep(scaled_cost, col_shift, log_mass_a, shrink, True, True, False)
        else:
            pot_col, weights = sweep(scaled_cost, col_shift, log_mass_a, shrink, True, False, True)
    pot_src = pot_col.reshape(rows)
    fin_fates = final_fates.astype(jnp.bfloat16)
    spread = lax.dynamic_update_slice_in_dim(
        jnp.zeros((fin_fates.shape[0], fin_width * tgt_count), jnp.bfloat16), fin_fates, tgt_rank * fin_width, 1
    )
    final_handed = lax.psum(spread, "tgt")
    handed = jnp.where(is_last, final_handed, jnp.zeros(final_handed.shape, jnp.bfloat16))
    fate_maps = jnp.zeros((final_fates.shape[0], rows), jnp.float32)
    for section_num in range(pair_count):
        active = pair_count - 1 - section_num
        pulled = lax.dot_general(
            handed, weights, (((1,), (1,)), ((), ())), preferred_element_type=jnp.float32
        )
        pulled = jnp.where(live_src[None, :], pulled, 0.0)
        fate_maps = jnp.where(pair_rank == active, pulled, fate_maps)
        if section_num + 1 < pair_count:
            passed = shifted(pulled.astype(jnp.bfloat16), "pair", -1)
            fresh = lax.all_gather(passed, ("src", "tgt"), axis=1, tiled=True)
            handed = jnp.where(pair_rank == active - 1, fresh, handed)
    pot_spread = lax.dynamic_update_slice_in_dim(jnp.zeros((src_width,), jnp.float32), pot_src, row_off, 0)
    pot_all = lax.psum(pot_spread, "tgt")
    return (fate_maps[None], pot_all[None])


def solution(mesh):
    placed = (P("pair", None, "src"), P(None, "tgt"), P("pair", "src"), P(), P(None, "tgt"))
    return jax.shard_map(
        local,
        mesh=mesh,
        in_specs=placed,
        out_specs=(P("pair", None, ("src", "tgt")), P("pair", "src")),
        check_vma=False,
    )
```

```python
import jax
import jax.numpy as jnp
from jax import lax
from jax.sharding import PartitionSpec as P
import functools
from jax.experimental import pallas as pl
from jax.experimental.pallas import tpu as pltpu

ITERS = 8


EPS = 0.1
LAM = 1.0
NEG = -1e30


GROUP = 16
ROW_GROUP = 128
WIDTH = 512


def sweep_kernel(do_row, do_col, emit_w, shrink, c_ref, b_ref, la_ref, *rest):
    rest = list(rest)
    f_ref = rest.pop(0) if do_row else None
    lse_ref = rest.pop(0) if do_col else None
    w_ref = rest.pop(0) if emit_w else None
    a_ref = rest.pop(0)
    rows, cols = c_ref.shape
    groups = rows // GROUP
    chunks = cols // WIDTH

    if do_row:
        rg = ROW_GROUP
        while rows % rg:
            rg //= 2

        def row_group(r, carry):
            rs = pl.ds(pl.multiple_of(r * rg, rg), rg)
            m = jnp.full((rg, WIDTH), -jnp.inf, jnp.float32)
            for j in range(chunks):
                cs = slice(j * WIDTH, (j + 1) * WIDTH)
                m = jnp.maximum(m, b_ref[:, cs] - c_ref[rs, cs])
            peak = jnp.max(m, axis=1, keepdims=True)
            s = jnp.zeros((rg, WIDTH), jnp.float32)
            for j in range(chunks):
                cs = slice(j * WIDTH, (j + 1) * WIDTH)
                s = s + jnp.exp(b_ref[:, cs] - c_ref[rs, cs] - peak)
            total = jnp.sum(s, axis=1, keepdims=True)
            pot = -shrink * EPS * (peak + jnp.log(total))
            f_ref[rs, :] = pot
            a_ref[rs, :] = jnp.broadcast_to(pot * (1.0 / EPS) + la_ref[rs, :], (rg, 128))
            if emit_w:
                for j in range(chunks):
                    cs = slice(j * WIDTH, (j + 1) * WIDTH)
                    e = jnp.exp(b_ref[:, cs] - c_ref[rs, cs] - peak)
                    w_ref[rs, cs] = (e / total).astype(w_ref.dtype)
            return carry
        lax.fori_loop(0, rows // rg, row_group, 0)
    else:
        a_ref[...] = jnp.broadcast_to(la_ref[...], a_ref.shape)

    if do_col:
        def col_chunk(j, carry):
            cs = pl.ds(pl.multiple_of(j * WIDTH, WIDTH), WIDTH)
            shifts = [jnp.tile(a_ref[r * GROUP:(r + 1) * GROUP, :], (1, WIDTH // 128))
                      for r in range(groups)]
            m = [jnp.full((GROUP, WIDTH), -jnp.inf, jnp.float32) for _ in range(2)]
            for r in range(groups):
                m[r % 2] = jnp.maximum(m[r % 2], shifts[r] - c_ref[r * GROUP:(r + 1) * GROUP, cs])
            peak = jnp.max(jnp.maximum(m[0], m[1]), axis=0, keepdims=True)
            s = [jnp.zeros((GROUP, WIDTH), jnp.float32) for _ in range(2)]
            for r in range(groups):
                s[r % 2] = s[r % 2] + jnp.exp(shifts[r] - c_ref[r * GROUP:(r + 1) * GROUP, cs] - peak)
            lse_ref[:, cs] = peak + jnp.log(jnp.sum(s[0] + s[1], axis=0, keepdims=True))
            return carry
        lax.fori_loop(0, chunks, col_chunk, 0)


def sweep(scaled_cost, col_shift, log_a, shrink, do_row, do_col, emit_w):
    rows, cols = scaled_cost.shape
    outs = []
    if do_row:
        outs.append(jax.ShapeDtypeStruct((rows, 1), jnp.float32))
    if do_col:
        outs.append(jax.ShapeDtypeStruct((1, cols), jnp.float32))
    if emit_w:
        outs.append(jax.ShapeDtypeStruct((rows, cols), jnp.bfloat16))
    passes = (2 if do_row else 0) + (2 if do_col else 0) + (1 if emit_w else 0)
    vmem = pl.BlockSpec(memory_space=pltpu.VMEM)
    return pl.pallas_call(
        functools.partial(sweep_kernel, do_row, do_col, emit_w, shrink),
        out_shape=tuple(outs),
        in_specs=[vmem] * 3,
        out_specs=tuple([vmem] * len(outs)),
        scratch_shapes=[pltpu.VMEM((rows, 128), jnp.float32)],
        compiler_params=pltpu.CompilerParams(vmem_limit_bytes=24 * 1024 * 1024),
        cost_estimate=pl.CostEstimate(
            flops=4 * passes * rows * cols,
            transcendentals=passes * rows * cols // 2,
            bytes_accessed=4 * rows * cols + (2 * rows * cols if emit_w else 0),
        ),
    )(scaled_cost, col_shift[None, :], log_a[:, None])


def shifted(shard, axis, by):
    devices = lax.axis_size(axis)
    pairs = [(i, i + by) for i in range(devices) if 0 <= i + by < devices]
    return lax.ppermute(shard, axis, pairs)


def local(src_cells, final_cells, growth, live, final_fates):
    pair_count = lax.axis_size("pair")
    tgt_count = lax.axis_size("tgt")
    pair_rank = lax.axis_index("pair")
    src_rank = lax.axis_index("src")
    tgt_rank = lax.axis_index("tgt")
    shrink = LAM / (LAM + EPS)
    source_all = src_cells[0]
    dims = source_all.shape[0]
    src_width = source_all.shape[1]
    rows = src_width // tgt_count
    row_off = tgt_rank * rows
    is_last = pair_rank == pair_count - 1
    source_pos = lax.dynamic_slice_in_dim(source_all, row_off, rows, 1)
    group = lax.axis_size("src") * tgt_count
    src_count = lax.axis_size("src")
    arrived = shifted(source_all, "pair", -1)
    mine_next = lax.dynamic_slice_in_dim(arrived, row_off, rows, 1)
    fin_width = final_cells.shape[1]
    mine_final = lax.dynamic_slice_in_dim(final_cells, (src_rank * rows) % fin_width, rows, 1)
    piece = jnp.where(is_last, mine_final, mine_next)
    pieces = lax.all_gather(piece, ("src", "tgt"))
    per_fin = fin_width // rows
    final_order = [
        (b % per_fin) * tgt_count + b // per_fin if per_fin == src_count else b for b in range(group)
    ]
    if per_fin == src_count:
        final_pieces = pieces[jnp.array(final_order, dtype=jnp.int32)]
        pieces = jnp.where(is_last, final_pieces, pieces)
        target_pos = jnp.transpose(pieces, (1, 0, 2)).reshape(dims, group * rows)
    else:
        final_all = lax.all_gather(final_cells, "tgt", axis=1, tiled=True)
        target_pos = jnp.where(
            is_last, final_all, jnp.transpose(pieces, (1, 0, 2)).reshape(dims, group * rows)
        )
    cols = target_pos.shape[1]
    cross = lax.dot_general(
        source_pos,
        target_pos,
        (((0,), (0,)), ((), ())),
        precision=lax.Precision.HIGHEST,
        preferred_element_type=jnp.float32,
    )
    src_sq = jnp.sum(source_pos * source_pos, axis=0)
    tgt_sq = jnp.sum(target_pos * target_pos, axis=0)
    cost_tile = (src_sq[:, None] + tgt_sq[None, :] - 2.0 * cross) / (2.0 * dims)
    live_now = lax.dynamic_index_in_dim(live, pair_rank, keepdims=False)
    live_next = lax.dynamic_index_in_dim(live, pair_rank + 1, keepdims=False)
    row_index = src_rank * src_width + row_off + jnp.arange(rows, dtype=jnp.int32)
    col_index = jnp.arange(cols, dtype=jnp.int32)
    live_src = row_index < live_now
    live_tgt = col_index < live_next
    growth_rows = lax.dynamic_slice_in_dim(growth[0], row_off, rows, 0)
    log_mass_a = jnp.where(
        live_src, jnp.log(growth_rows) - jnp.log(live_now.astype(jnp.float32)), NEG
    )
    log_mass_b = jnp.where(
        live_tgt, -jnp.log(live_next.astype(jnp.float32)) * jnp.ones((cols,), jnp.float32), NEG
    )
    scaled_cost = cost_tile * (1.0 / EPS)
    (part_lse,) = sweep(scaled_cost, log_mass_b, log_mass_a, shrink, False, True, False)
    for step_num in range(ITERS):
        every = lax.all_gather(part_lse[0], ("src", "tgt"))
        every_peak = jnp.max(every, axis=0)
        col_lse = every_peak + jnp.log(jnp.sum(jnp.exp(every - every_peak[None, :]), axis=0))
        pot_tgt = -shrink * EPS * col_lse
        col_shift = pot_tgt * (1.0 / EPS) + log_mass_b
        if step_num + 1 < ITERS:
            pot_col, part_lse = sweep(scaled_cost, col_shift, log_mass_a, shrink, True, True, False)
        else:
            pot_col, weights = sweep(scaled_cost, col_shift, log_mass_a, shrink, True, False, True)
    pot_src = pot_col.reshape(rows)
    final_handed = lax.all_gather(final_fates.astype(jnp.bfloat16), "tgt", axis=1, tiled=True)
    handed = jnp.where(is_last, final_handed, jnp.zeros(final_handed.shape, jnp.bfloat16))
    fate_maps = jnp.zeros((final_fates.shape[0], rows), jnp.float32)
    for section_num in range(pair_count):
        active = pair_count - 1 - section_num
        pulled = lax.dot_general(
            handed, weights, (((1,), (1,)), ((), ())), preferred_element_type=jnp.float32
        )
        pulled = jnp.where(live_src[None, :], pulled, 0.0)
        fate_maps = jnp.where(pair_rank == active, pulled, fate_maps)
        if section_num + 1 < pair_count:
            passed = shifted(pulled.astype(jnp.bfloat16), "pair", -1)
            fresh = lax.all_gather(passed, ("src", "tgt"), axis=1, tiled=True)
            handed = jnp.where(pair_rank == active - 1, fresh, handed)
    pot_spread = lax.dynamic_update_slice_in_dim(jnp.zeros((src_width,), jnp.float32), pot_src, row_off, 0)
    pot_all = lax.psum(pot_spread, "tgt")
    return (fate_maps[None], pot_all[None])


def solution(mesh):
    placed = (P("pair", None, "src"), P(None, "tgt"), P("pair", "src"), P(), P(None, "tgt"))
    return jax.shard_map(
        local,
        mesh=mesh,
        in_specs=placed,
        out_specs=(P("pair", None, ("src", "tgt")), P("pair", "src")),
        check_vma=False,
    )
```

```python
import jax
import jax.numpy as jnp
from jax import lax
from jax.sharding import PartitionSpec as P
import functools
from jax.experimental import pallas as pl
from jax.experimental.pallas import tpu as pltpu

ITERS = 8


EPS = 0.1
LAM = 1.0
NEG = -1e30


GROUP = 16
ROW_GROUP = 128
WIDTH = 512


def sweep_kernel(do_row, do_col, emit_w, shrink, c_ref, every_ref, lb_ref, la_ref, *rest):
    rest = list(rest)
    f_ref = rest.pop(0) if do_row else None
    lse_ref = rest.pop(0) if do_col else None
    w_ref = rest.pop(0) if emit_w else None
    a_ref, b_ref = rest
    rows, cols = c_ref.shape
    groups = rows // GROUP
    chunks = cols // WIDTH

    if do_row:
        for j in range(chunks):
            cs = slice(j * WIDTH, (j + 1) * WIDTH)
            ev = every_ref[:, cs]
            top = jnp.max(ev, axis=0, keepdims=True)
            col_lse = top + jnp.log(jnp.sum(jnp.exp(ev - top), axis=0, keepdims=True))
            b_ref[:, cs] = (-shrink * EPS * col_lse) * (1.0 / EPS) + lb_ref[:, cs]
        rg = ROW_GROUP
        while rows % rg:
            rg //= 2

        def row_group(r, carry):
            rs = pl.ds(pl.multiple_of(r * rg, rg), rg)
            m = jnp.full((rg, WIDTH), -jnp.inf, jnp.float32)
            for j in range(chunks):
                cs = slice(j * WIDTH, (j + 1) * WIDTH)
                m = jnp.maximum(m, b_ref[:, cs] - c_ref[rs, cs])
            peak = jnp.max(m, axis=1, keepdims=True)
            s = jnp.zeros((rg, WIDTH), jnp.float32)
            for j in range(chunks):
                cs = slice(j * WIDTH, (j + 1) * WIDTH)
                s = s + jnp.exp(b_ref[:, cs] - c_ref[rs, cs] - peak)
            total = jnp.sum(s, axis=1, keepdims=True)
            pot = -shrink * EPS * (peak + jnp.log(total))
            f_ref[rs, :] = pot
            a_ref[rs, :] = jnp.broadcast_to(pot * (1.0 / EPS) + la_ref[rs, :], (rg, 128))
            if emit_w:
                for j in range(chunks):
                    cs = slice(j * WIDTH, (j + 1) * WIDTH)
                    e = jnp.exp(b_ref[:, cs] - c_ref[rs, cs] - peak)
                    w_ref[rs, cs] = (e / total).astype(w_ref.dtype)
            return carry
        lax.fori_loop(0, rows // rg, row_group, 0)
    else:
        a_ref[...] = jnp.broadcast_to(la_ref[...], a_ref.shape)

    if do_col:
        def col_chunk(j, carry):
            cs = pl.ds(pl.multiple_of(j * WIDTH, WIDTH), WIDTH)
            shifts = [jnp.tile(a_ref[r * GROUP:(r + 1) * GROUP, :], (1, WIDTH // 128))
                      for r in range(groups)]
            m = [jnp.full((GROUP, WIDTH), -jnp.inf, jnp.float32) for _ in range(2)]
            for r in range(groups):
                m[r % 2] = jnp.maximum(m[r % 2], shifts[r] - c_ref[r * GROUP:(r + 1) * GROUP, cs])
            peak = jnp.max(jnp.maximum(m[0], m[1]), axis=0, keepdims=True)
            s = [jnp.zeros((GROUP, WIDTH), jnp.float32) for _ in range(2)]
            for r in range(groups):
                s[r % 2] = s[r % 2] + jnp.exp(shifts[r] - c_ref[r * GROUP:(r + 1) * GROUP, cs] - peak)
            lse_ref[:, cs] = peak + jnp.log(jnp.sum(s[0] + s[1], axis=0, keepdims=True))
            return carry
        lax.fori_loop(0, chunks, col_chunk, 0)


def sweep(scaled_cost, every, log_b, log_a, shrink, do_row, do_col, emit_w):
    rows, cols = scaled_cost.shape
    outs = []
    if do_row:
        outs.append(jax.ShapeDtypeStruct((rows, 1), jnp.float32))
    if do_col:
        outs.append(jax.ShapeDtypeStruct((1, cols), jnp.float32))
    if emit_w:
        outs.append(jax.ShapeDtypeStruct((rows, cols), jnp.bfloat16))
    passes = (2 if do_row else 0) + (2 if do_col else 0) + (1 if emit_w else 0)
    vmem = pl.BlockSpec(memory_space=pltpu.VMEM)
    return pl.pallas_call(
        functools.partial(sweep_kernel, do_row, do_col, emit_w, shrink),
        out_shape=tuple(outs),
        in_specs=[vmem] * 4,
        out_specs=tuple([vmem] * len(outs)),
        scratch_shapes=[pltpu.VMEM((rows, 128), jnp.float32), pltpu.VMEM((1, cols), jnp.float32)],
        compiler_params=pltpu.CompilerParams(vmem_limit_bytes=24 * 1024 * 1024),
        cost_estimate=pl.CostEstimate(
            flops=4 * passes * rows * cols,
            transcendentals=passes * rows * cols // 2,
            bytes_accessed=4 * rows * cols + (2 * rows * cols if emit_w else 0),
        ),
    )(scaled_cost, every, log_b[None, :], log_a[:, None])


def shifted(shard, axis, by):
    devices = lax.axis_size(axis)
    pairs = [(i, i + by) for i in range(devices) if 0 <= i + by < devices]
    return lax.ppermute(shard, axis, pairs)


def local(src_cells, final_cells, growth, live, final_fates):
    pair_count = lax.axis_size("pair")
    tgt_count = lax.axis_size("tgt")
    pair_rank = lax.axis_index("pair")
    src_rank = lax.axis_index("src")
    tgt_rank = lax.axis_index("tgt")
    shrink = LAM / (LAM + EPS)
    source_all = src_cells[0]
    dims = source_all.shape[0]
    src_width = source_all.shape[1]
    rows = src_width // tgt_count
    row_off = tgt_rank * rows
    is_last = pair_rank == pair_count - 1
    source_pos = lax.dynamic_slice_in_dim(source_all, row_off, rows, 1)
    group = lax.axis_size("src") * tgt_count
    src_count = lax.axis_size("src")
    arrived = shifted(source_all, "pair", -1)
    mine_next = lax.dynamic_slice_in_dim(arrived, row_off, rows, 1)
    fin_width = final_cells.shape[1]
    mine_final = lax.dynamic_slice_in_dim(final_cells, (src_rank * rows) % fin_width, rows, 1)
    piece = jnp.where(is_last, mine_final, mine_next)
    pieces = lax.all_gather(piece, ("src", "tgt"))
    per_fin = fin_width // rows
    final_order = [
        (b % per_fin) * tgt_count + b // per_fin if per_fin == src_count else b for b in range(group)
    ]
    if per_fin == src_count:
        final_pieces = pieces[jnp.array(final_order, dtype=jnp.int32)]
        pieces = jnp.where(is_last, final_pieces, pieces)
        target_pos = jnp.transpose(pieces, (1, 0, 2)).reshape(dims, group * rows)
    else:
        final_all = lax.all_gather(final_cells, "tgt", axis=1, tiled=True)
        target_pos = jnp.where(
            is_last, final_all, jnp.transpose(pieces, (1, 0, 2)).reshape(dims, group * rows)
        )
    cols = target_pos.shape[1]
    cross = lax.dot_general(
        source_pos,
        target_pos,
        (((0,), (0,)), ((), ())),
        precision=lax.Precision.HIGHEST,
        preferred_element_type=jnp.float32,
    )
    src_sq = jnp.sum(source_pos * source_pos, axis=0)
    tgt_sq = jnp.sum(target_pos * target_pos, axis=0)
    cost_tile = (src_sq[:, None] + tgt_sq[None, :] - 2.0 * cross) / (2.0 * dims)
    live_now = lax.dynamic_index_in_dim(live, pair_rank, keepdims=False)
    live_next = lax.dynamic_index_in_dim(live, pair_rank + 1, keepdims=False)
    row_index = src_rank * src_width + row_off + jnp.arange(rows, dtype=jnp.int32)
    col_index = jnp.arange(cols, dtype=jnp.int32)
    live_src = row_index < live_now
    live_tgt = col_index < live_next
    growth_rows = lax.dynamic_slice_in_dim(growth[0], row_off, rows, 0)
    log_mass_a = jnp.where(
        live_src, jnp.log(growth_rows) - jnp.log(live_now.astype(jnp.float32)), NEG
    )
    log_mass_b = jnp.where(
        live_tgt, -jnp.log(live_next.astype(jnp.float32)) * jnp.ones((cols,), jnp.float32), NEG
    )
    scaled_cost = cost_tile * (1.0 / EPS)
    (part_lse,) = sweep(scaled_cost, log_mass_b[None, :], log_mass_b, log_mass_a, shrink, False, True, False)
    for step_num in range(ITERS):
        every = lax.all_gather(part_lse[0], ("src", "tgt"))
        if step_num + 1 < ITERS:
            pot_col, part_lse = sweep(scaled_cost, every, log_mass_b, log_mass_a, shrink, True, True, False)
        else:
            pot_col, weights = sweep(scaled_cost, every, log_mass_b, log_mass_a, shrink, True, False, True)
    pot_src = pot_col.reshape(rows)
    final_handed = lax.all_gather(final_fates.astype(jnp.bfloat16), "tgt", axis=1, tiled=True)
    handed = jnp.where(is_last, final_handed, jnp.zeros(final_handed.shape, jnp.bfloat16))
    fate_maps = jnp.zeros((final_fates.shape[0], rows), jnp.float32)
    for section_num in range(pair_count):
        active = pair_count - 1 - section_num
        pulled = lax.dot_general(
            weights, handed, (((1,), (1,)), ((), ())), preferred_element_type=jnp.float32
        ).T
        pulled = jnp.where(live_src[None, :], pulled, 0.0)
        fate_maps = jnp.where(pair_rank == active, pulled, fate_maps)
        if section_num + 1 < pair_count:
            passed = shifted(pulled.astype(jnp.bfloat16), "pair", -1)
            fresh = lax.all_gather(passed, ("src", "tgt"), axis=1, tiled=True)
            handed = jnp.where(pair_rank == active - 1, fresh, handed)
    pot_spread = lax.dynamic_update_slice_in_dim(jnp.zeros((src_width,), jnp.float32), pot_src, row_off, 0)
    pot_all = lax.psum(pot_spread, "tgt")
    return (fate_maps[None], pot_all[None])


def solution(mesh):
    placed = (P("pair", None, "src"), P(None, "tgt"), P("pair", "src"), P(), P(None, "tgt"))
    return jax.shard_map(
        local,
        mesh=mesh,
        in_specs=placed,
        out_specs=(P("pair", None, ("src", "tgt")), P("pair", "src")),
        check_vma=False,
    )
```

```python
import jax
import jax.numpy as jnp
from jax import lax
from jax.sharding import PartitionSpec as P
import functools
from jax.experimental import pallas as pl
from jax.experimental.pallas import tpu as pltpu

ITERS = 8


EPS = 0.1
LAM = 1.0
NEG = -1e30


GROUP = 16
ROW_GROUP = 128
WIDTH = 512


def sweep_kernel(do_row, do_col, emit_w, shrink, c_ref, every_ref, lb_ref, la_ref, *rest):
    rest = list(rest)
    f_ref = rest.pop(0) if do_row else None
    lse_ref = rest.pop(0) if do_col else None
    w_ref = rest.pop(0) if emit_w else None
    a_ref, b_ref = rest
    rows, cols = c_ref.shape
    groups = rows // GROUP
    chunks = cols // WIDTH

    if do_row:
        for j in range(chunks):
            cs = slice(j * WIDTH, (j + 1) * WIDTH)
            ev = every_ref[:, cs]
            top = jnp.max(ev, axis=0, keepdims=True)
            col_lse = top + jnp.log(jnp.sum(jnp.exp(ev - top), axis=0, keepdims=True))
            b_ref[:, cs] = (-shrink * EPS * col_lse) * (1.0 / EPS) + lb_ref[:, cs]
        rg = ROW_GROUP
        while rows % rg:
            rg //= 2

        def row_group(r, carry):
            rs = pl.ds(pl.multiple_of(r * rg, rg), rg)
            m = jnp.full((rg, WIDTH), -jnp.inf, jnp.float32)
            for j in range(chunks):
                cs = slice(j * WIDTH, (j + 1) * WIDTH)
                m = jnp.maximum(m, b_ref[:, cs] - c_ref[rs, cs])
            peak = jnp.max(m, axis=1, keepdims=True)
            s = jnp.zeros((rg, WIDTH), jnp.float32)
            for j in range(chunks):
                cs = slice(j * WIDTH, (j + 1) * WIDTH)
                s = s + jnp.exp(b_ref[:, cs] - c_ref[rs, cs] - peak)
            total = jnp.sum(s, axis=1, keepdims=True)
            pot = -shrink * EPS * (peak + jnp.log(total))
            f_ref[rs, :] = pot
            a_ref[rs, :] = jnp.broadcast_to(pot * (1.0 / EPS) + la_ref[rs, :], (rg, 128))
            if emit_w:
                for j in range(chunks):
                    cs = slice(j * WIDTH, (j + 1) * WIDTH)
                    e = jnp.exp(b_ref[:, cs] - c_ref[rs, cs] - peak)
                    w_ref[rs, cs] = (e / total).astype(w_ref.dtype)
            return carry
        lax.fori_loop(0, rows // rg, row_group, 0)
    else:
        a_ref[...] = jnp.broadcast_to(la_ref[...], a_ref.shape)

    if do_col:
        def col_chunk(j, carry):
            cs = pl.ds(pl.multiple_of(j * WIDTH, WIDTH), WIDTH)
            shifts = [jnp.tile(a_ref[r * GROUP:(r + 1) * GROUP, :], (1, WIDTH // 128))
                      for r in range(groups)]
            m = [jnp.full((GROUP, WIDTH), -jnp.inf, jnp.float32) for _ in range(2)]
            for r in range(groups):
                m[r % 2] = jnp.maximum(m[r % 2], shifts[r] - c_ref[r * GROUP:(r + 1) * GROUP, cs])
            peak = jnp.max(jnp.maximum(m[0], m[1]), axis=0, keepdims=True)
            s = [jnp.zeros((GROUP, WIDTH), jnp.float32) for _ in range(2)]
            for r in range(groups):
                s[r % 2] = s[r % 2] + jnp.exp(shifts[r] - c_ref[r * GROUP:(r + 1) * GROUP, cs] - peak)
            lse_ref[:, cs] = peak + jnp.log(jnp.sum(s[0] + s[1], axis=0, keepdims=True))
            return carry
        lax.fori_loop(0, chunks, col_chunk, 0)


def sweep(scaled_cost, every, log_b, log_a, shrink, do_row, do_col, emit_w):
    rows, cols = scaled_cost.shape
    outs = []
    if do_row:
        outs.append(jax.ShapeDtypeStruct((rows, 1), jnp.float32))
    if do_col:
        outs.append(jax.ShapeDtypeStruct((1, cols), jnp.float32))
    if emit_w:
        outs.append(jax.ShapeDtypeStruct((rows, cols), jnp.bfloat16))
    passes = (2 if do_row else 0) + (2 if do_col else 0) + (1 if emit_w else 0)
    vmem = pl.BlockSpec(memory_space=pltpu.VMEM)
    return pl.pallas_call(
        functools.partial(sweep_kernel, do_row, do_col, emit_w, shrink),
        out_shape=tuple(outs),
        in_specs=[vmem] * 4,
        out_specs=tuple([vmem] * len(outs)),
        scratch_shapes=[pltpu.VMEM((rows, 128), jnp.float32), pltpu.VMEM((1, cols), jnp.float32)],
        compiler_params=pltpu.CompilerParams(vmem_limit_bytes=24 * 1024 * 1024),
        cost_estimate=pl.CostEstimate(
            flops=4 * passes * rows * cols,
            transcendentals=passes * rows * cols // 2,
            bytes_accessed=4 * rows * cols + (2 * rows * cols if emit_w else 0),
        ),
    )(scaled_cost, every, log_b[None, :], log_a[:, None])


def shifted(shard, axis, by):
    devices = lax.axis_size(axis)
    pairs = [(i, i + by) for i in range(devices) if 0 <= i + by < devices]
    return lax.ppermute(shard, axis, pairs)


def local(src_cells, final_cells, growth, live, final_fates):
    pair_count = lax.axis_size("pair")
    tgt_count = lax.axis_size("tgt")
    pair_rank = lax.axis_index("pair")
    src_rank = lax.axis_index("src")
    tgt_rank = lax.axis_index("tgt")
    shrink = LAM / (LAM + EPS)
    source_all = src_cells[0]
    dims = source_all.shape[0]
    src_width = source_all.shape[1]
    rows = src_width // tgt_count
    row_off = tgt_rank * rows
    is_last = pair_rank == pair_count - 1
    source_pos = lax.dynamic_slice_in_dim(source_all, row_off, rows, 1)
    group = lax.axis_size("src") * tgt_count
    src_count = lax.axis_size("src")
    arrived = shifted(source_all, "pair", -1)
    mine_next = lax.dynamic_slice_in_dim(arrived, row_off, rows, 1)
    fin_width = final_cells.shape[1]
    mine_final = lax.dynamic_slice_in_dim(final_cells, (src_rank * rows) % fin_width, rows, 1)
    piece = jnp.where(is_last, mine_final, mine_next)
    fates_count = final_fates.shape[0]
    per_fin = fin_width // rows
    final_order = [(b % per_fin) * tgt_count + b // per_fin for b in range(group)]
    if per_fin == src_count:
        fate_piece = lax.dynamic_slice_in_dim(final_fates, src_rank * rows, rows, 1)
        fate_piece = fate_piece.astype(jnp.bfloat16).astype(jnp.float32)
        pieces = lax.all_gather(jnp.concatenate([piece, fate_piece], axis=0), ("src", "tgt"))
        final_pieces = pieces[jnp.array(final_order, dtype=jnp.int32)]
        cell_pieces = jnp.where(is_last, final_pieces[:, :dims], pieces[:, :dims])
        target_pos = jnp.transpose(cell_pieces, (1, 0, 2)).reshape(dims, group * rows)
        final_handed = (
            jnp.transpose(final_pieces[:, dims:], (1, 0, 2))
            .reshape(fates_count, group * rows)
            .astype(jnp.bfloat16)
        )
    else:
        pieces = lax.all_gather(piece, ("src", "tgt"))
        final_all = lax.all_gather(final_cells, "tgt", axis=1, tiled=True)
        target_pos = jnp.where(
            is_last, final_all, jnp.transpose(pieces, (1, 0, 2)).reshape(dims, group * rows)
        )
        final_handed = lax.all_gather(final_fates.astype(jnp.bfloat16), "tgt", axis=1, tiled=True)
    cols = target_pos.shape[1]
    cross = lax.dot_general(
        source_pos,
        target_pos,
        (((0,), (0,)), ((), ())),
        precision=lax.Precision.HIGHEST,
        preferred_element_type=jnp.float32,
    )
    src_sq = jnp.sum(source_pos * source_pos, axis=0)
    tgt_sq = jnp.sum(target_pos * target_pos, axis=0)
    cost_tile = (src_sq[:, None] + tgt_sq[None, :] - 2.0 * cross) / (2.0 * dims)
    live_now = lax.dynamic_index_in_dim(live, pair_rank, keepdims=False)
    live_next = lax.dynamic_index_in_dim(live, pair_rank + 1, keepdims=False)
    row_index = src_rank * src_width + row_off + jnp.arange(rows, dtype=jnp.int32)
    col_index = jnp.arange(cols, dtype=jnp.int32)
    live_src = row_index < live_now
    live_tgt = col_index < live_next
    growth_rows = lax.dynamic_slice_in_dim(growth[0], row_off, rows, 0)
    log_mass_a = jnp.where(
        live_src, jnp.log(growth_rows) - jnp.log(live_now.astype(jnp.float32)), NEG
    )
    log_mass_b = jnp.where(
        live_tgt, -jnp.log(live_next.astype(jnp.float32)) * jnp.ones((cols,), jnp.float32), NEG
    )
    scaled_cost = cost_tile * (1.0 / EPS)
    (part_lse,) = sweep(scaled_cost, log_mass_b[None, :], log_mass_b, log_mass_a, shrink, False, True, False)
    for step_num in range(ITERS):
        every = lax.all_gather(part_lse[0], ("src", "tgt"))
        if step_num + 1 < ITERS:
            pot_col, part_lse = sweep(scaled_cost, every, log_mass_b, log_mass_a, shrink, True, True, False)
        else:
            pot_col, weights = sweep(scaled_cost, every, log_mass_b, log_mass_a, shrink, True, False, True)
    pot_src = pot_col.reshape(rows)
    handed = jnp.where(is_last, final_handed, jnp.zeros(final_handed.shape, jnp.bfloat16))
    fate_maps = jnp.zeros((final_fates.shape[0], rows), jnp.float32)
    for section_num in range(pair_count):
        active = pair_count - 1 - section_num
        pulled = lax.dot_general(
            weights, handed, (((1,), (1,)), ((), ())), preferred_element_type=jnp.float32
        ).T
        pulled = jnp.where(live_src[None, :], pulled, 0.0)
        fate_maps = jnp.where(pair_rank == active, pulled, fate_maps)
        if section_num + 1 < pair_count:
            passed = shifted(pulled.astype(jnp.bfloat16), "pair", -1)
            fresh = lax.all_gather(passed, ("src", "tgt"), axis=1, tiled=True)
            handed = jnp.where(pair_rank == active - 1, fresh, handed)
    pot_spread = lax.dynamic_update_slice_in_dim(jnp.zeros((src_width,), jnp.float32), pot_src, row_off, 0)
    pot_all = lax.psum(pot_spread, "tgt")
    return (fate_maps[None], pot_all[None])


def solution(mesh):
    placed = (P("pair", None, "src"), P(None, "tgt"), P("pair", "src"), P(), P(None, "tgt"))
    return jax.shard_map(
        local,
        mesh=mesh,
        in_specs=placed,
        out_specs=(P("pair", None, ("src", "tgt")), P("pair", "src")),
        check_vma=False,
    )
```

```python
import jax
import jax.numpy as jnp
from jax import lax
from jax.sharding import PartitionSpec as P
import functools
from jax.experimental import pallas as pl
from jax.experimental.pallas import tpu as pltpu

ITERS = 8


EPS = 0.1
LAM = 1.0
NEG = -1e30


GROUP = 16
ROW_GROUP = 128
WIDTH = 512


def sweep_kernel(do_row, do_col, emit_w, shrink, c_ref, every_ref, lb_ref, la_ref, *rest):
    rest = list(rest)
    handed_ref = rest.pop(0) if emit_w else None
    f_ref = rest.pop(0) if do_row else None
    lse_ref = rest.pop(0) if do_col else None
    w_ref = rest.pop(0) if emit_w else None
    p_ref = rest.pop(0) if emit_w else None
    a_ref, b_ref = rest
    rows, cols = c_ref.shape
    groups = rows // GROUP
    chunks = cols // WIDTH

    if do_row:
        for j in range(chunks):
            cs = slice(j * WIDTH, (j + 1) * WIDTH)
            ev = every_ref[:, cs]
            top = jnp.max(ev, axis=0, keepdims=True)
            col_lse = top + jnp.log(jnp.sum(jnp.exp(ev - top), axis=0, keepdims=True))
            b_ref[:, cs] = (-shrink * EPS * col_lse) * (1.0 / EPS) + lb_ref[:, cs]
        rg = ROW_GROUP
        while rows % rg:
            rg //= 2

        def row_group(r, carry):
            rs = pl.ds(pl.multiple_of(r * rg, rg), rg)
            m = jnp.full((rg, WIDTH), -jnp.inf, jnp.float32)
            for j in range(chunks):
                cs = slice(j * WIDTH, (j + 1) * WIDTH)
                m = jnp.maximum(m, b_ref[:, cs] - c_ref[rs, cs])
            peak = jnp.max(m, axis=1, keepdims=True)
            s = jnp.zeros((rg, WIDTH), jnp.float32)
            for j in range(chunks):
                cs = slice(j * WIDTH, (j + 1) * WIDTH)
                s = s + jnp.exp(b_ref[:, cs] - c_ref[rs, cs] - peak)
            total = jnp.sum(s, axis=1, keepdims=True)
            pot = -shrink * EPS * (peak + jnp.log(total))
            f_ref[rs, :] = pot
            a_ref[rs, :] = jnp.broadcast_to(pot * (1.0 / EPS) + la_ref[rs, :], (rg, 128))
            if emit_w:
                for j in range(chunks):
                    cs = slice(j * WIDTH, (j + 1) * WIDTH)
                    e = jnp.exp(b_ref[:, cs] - c_ref[rs, cs] - peak)
                    w_ref[rs, cs] = (e / total).astype(w_ref.dtype)
                p_ref[:, rs] = lax.dot_general(
                    handed_ref[...], w_ref[rs, :], (((1,), (1,)), ((), ())),
                    preferred_element_type=jnp.float32,
                )
            return carry
        lax.fori_loop(0, rows // rg, row_group, 0)
    else:
        a_ref[...] = jnp.broadcast_to(la_ref[...], a_ref.shape)

    if do_col:
        def col_chunk(j, carry):
            cs = pl.ds(pl.multiple_of(j * WIDTH, WIDTH), WIDTH)
            shifts = [jnp.tile(a_ref[r * GROUP:(r + 1) * GROUP, :], (1, WIDTH // 128))
                      for r in range(groups)]
            m = [jnp.full((GROUP, WIDTH), -jnp.inf, jnp.float32) for _ in range(2)]
            for r in range(groups):
                m[r % 2] = jnp.maximum(m[r % 2], shifts[r] - c_ref[r * GROUP:(r + 1) * GROUP, cs])
            peak = jnp.max(jnp.maximum(m[0], m[1]), axis=0, keepdims=True)
            s = [jnp.zeros((GROUP, WIDTH), jnp.float32) for _ in range(2)]
            for r in range(groups):
                s[r % 2] = s[r % 2] + jnp.exp(shifts[r] - c_ref[r * GROUP:(r + 1) * GROUP, cs] - peak)
            lse_ref[:, cs] = peak + jnp.log(jnp.sum(s[0] + s[1], axis=0, keepdims=True))
            return carry
        lax.fori_loop(0, chunks, col_chunk, 0)


def sweep(scaled_cost, every, log_b, log_a, shrink, do_row, do_col, emit_w, handed=None):
    rows, cols = scaled_cost.shape
    outs = []
    if do_row:
        outs.append(jax.ShapeDtypeStruct((rows, 1), jnp.float32))
    if do_col:
        outs.append(jax.ShapeDtypeStruct((1, cols), jnp.float32))
    if emit_w:
        outs.append(jax.ShapeDtypeStruct((rows, cols), jnp.bfloat16))
        outs.append(jax.ShapeDtypeStruct((handed.shape[0], rows), jnp.float32))
    passes = (2 if do_row else 0) + (2 if do_col else 0) + (1 if emit_w else 0)
    vmem = pl.BlockSpec(memory_space=pltpu.VMEM)
    return pl.pallas_call(
        functools.partial(sweep_kernel, do_row, do_col, emit_w, shrink),
        out_shape=tuple(outs),
        in_specs=[vmem] * (5 if emit_w else 4),
        out_specs=tuple([vmem] * len(outs)),
        scratch_shapes=[pltpu.VMEM((rows, 128), jnp.float32), pltpu.VMEM((1, cols), jnp.float32)],
        compiler_params=pltpu.CompilerParams(vmem_limit_bytes=24 * 1024 * 1024),
        cost_estimate=pl.CostEstimate(
            flops=4 * passes * rows * cols,
            transcendentals=passes * rows * cols // 2,
            bytes_accessed=4 * rows * cols + (2 * rows * cols if emit_w else 0),
        ),
    )(scaled_cost, every, log_b[None, :], log_a[:, None], *([handed] if emit_w else []))


def shifted(shard, axis, by):
    devices = lax.axis_size(axis)
    pairs = [(i, i + by) for i in range(devices) if 0 <= i + by < devices]
    return lax.ppermute(shard, axis, pairs)


def local(src_cells, final_cells, growth, live, final_fates):
    pair_count = lax.axis_size("pair")
    tgt_count = lax.axis_size("tgt")
    pair_rank = lax.axis_index("pair")
    src_rank = lax.axis_index("src")
    tgt_rank = lax.axis_index("tgt")
    shrink = LAM / (LAM + EPS)
    source_all = src_cells[0]
    dims = source_all.shape[0]
    src_width = source_all.shape[1]
    rows = src_width // tgt_count
    row_off = tgt_rank * rows
    is_last = pair_rank == pair_count - 1
    source_pos = lax.dynamic_slice_in_dim(source_all, row_off, rows, 1)
    group = lax.axis_size("src") * tgt_count
    src_count = lax.axis_size("src")
    arrived = shifted(source_all, "pair", -1)
    mine_next = lax.dynamic_slice_in_dim(arrived, row_off, rows, 1)
    fin_width = final_cells.shape[1]
    mine_final = lax.dynamic_slice_in_dim(final_cells, (src_rank * rows) % fin_width, rows, 1)
    piece = jnp.where(is_last, mine_final, mine_next)
    pieces = lax.all_gather(piece, ("src", "tgt"))
    per_fin = fin_width // rows
    final_order = [
        (b % per_fin) * tgt_count + b // per_fin if per_fin == src_count else b for b in range(group)
    ]
    if per_fin == src_count:
        final_pieces = pieces[jnp.array(final_order, dtype=jnp.int32)]
        pieces = jnp.where(is_last, final_pieces, pieces)
        target_pos = jnp.transpose(pieces, (1, 0, 2)).reshape(dims, group * rows)
    else:
        final_all = lax.all_gather(final_cells, "tgt", axis=1, tiled=True)
        target_pos = jnp.where(
            is_last, final_all, jnp.transpose(pieces, (1, 0, 2)).reshape(dims, group * rows)
        )
    cols = target_pos.shape[1]
    cross = lax.dot_general(
        source_pos,
        target_pos,
        (((0,), (0,)), ((), ())),
        precision=lax.Precision.HIGHEST,
        preferred_element_type=jnp.float32,
    )
    src_sq = jnp.sum(source_pos * source_pos, axis=0)
    tgt_sq = jnp.sum(target_pos * target_pos, axis=0)
    cost_tile = (src_sq[:, None] + tgt_sq[None, :] - 2.0 * cross) / (2.0 * dims)
    live_now = lax.dynamic_index_in_dim(live, pair_rank, keepdims=False)
    live_next = lax.dynamic_index_in_dim(live, pair_rank + 1, keepdims=False)
    row_index = src_rank * src_width + row_off + jnp.arange(rows, dtype=jnp.int32)
    col_index = jnp.arange(cols, dtype=jnp.int32)
    live_src = row_index < live_now
    live_tgt = col_index < live_next
    growth_rows = lax.dynamic_slice_in_dim(growth[0], row_off, rows, 0)
    log_mass_a = jnp.where(
        live_src, jnp.log(growth_rows) - jnp.log(live_now.astype(jnp.float32)), NEG
    )
    log_mass_b = jnp.where(
        live_tgt, -jnp.log(live_next.astype(jnp.float32)) * jnp.ones((cols,), jnp.float32), NEG
    )
    scaled_cost = cost_tile * (1.0 / EPS)
    final_handed = lax.all_gather(final_fates.astype(jnp.bfloat16), "tgt", axis=1, tiled=True)
    fates_count = final_handed.shape[0]
    fates_pad = -fates_count % 16
    handed_pad = jnp.concatenate(
        [final_handed, jnp.zeros((fates_pad, final_handed.shape[1]), jnp.bfloat16)], axis=0
    )
    (part_lse,) = sweep(scaled_cost, log_mass_b[None, :], log_mass_b, log_mass_a, shrink, False, True, False)
    for step_num in range(ITERS):
        every = lax.all_gather(part_lse[0], ("src", "tgt"))
        if step_num + 1 < ITERS:
            pot_col, part_lse = sweep(scaled_cost, every, log_mass_b, log_mass_a, shrink, True, True, False)
        else:
            pot_col, weights, first_pull = sweep(
                scaled_cost, every, log_mass_b, log_mass_a, shrink, True, False, True, handed_pad
            )
    pot_src = pot_col.reshape(rows)
    handed = jnp.where(is_last, final_handed, jnp.zeros(final_handed.shape, jnp.bfloat16))
    fate_maps = jnp.zeros((final_fates.shape[0], rows), jnp.float32)
    for section_num in range(pair_count):
        active = pair_count - 1 - section_num
        if section_num == 0:
            pulled = first_pull[:fates_count]
        else:
            pulled = lax.dot_general(
                weights, handed, (((1,), (1,)), ((), ())), preferred_element_type=jnp.float32
            ).T
        pulled = jnp.where(live_src[None, :], pulled, 0.0)
        fate_maps = jnp.where(pair_rank == active, pulled, fate_maps)
        if section_num + 1 < pair_count:
            passed = shifted(pulled.astype(jnp.bfloat16), "pair", -1)
            fresh = lax.all_gather(passed, ("src", "tgt"), axis=1, tiled=True)
            handed = jnp.where(pair_rank == active - 1, fresh, handed)
    pot_spread = lax.dynamic_update_slice_in_dim(jnp.zeros((src_width,), jnp.float32), pot_src, row_off, 0)
    pot_all = lax.psum(pot_spread, "tgt")
    return (fate_maps[None], pot_all[None])


def solution(mesh):
    placed = (P("pair", None, "src"), P(None, "tgt"), P("pair", "src"), P(), P(None, "tgt"))
    return jax.shard_map(
        local,
        mesh=mesh,
        in_specs=placed,
        out_specs=(P("pair", None, ("src", "tgt")), P("pair", "src")),
        check_vma=False,
    )
```

```python
import jax
import jax.numpy as jnp
from jax import lax
from jax.sharding import PartitionSpec as P
import functools
from jax.experimental import pallas as pl
from jax.experimental.pallas import tpu as pltpu

ITERS = 8


EPS = 0.1
LAM = 1.0
NEG = -1e30


GROUP = 16
ROW_GROUP = 128
WIDTH = 512


def sweep_kernel(do_row, do_col, emit_w, shrink, c_ref, every_ref, lb_ref, la_ref, *rest):
    rest = list(rest)
    handed_ref = rest.pop(0) if emit_w else None
    f_ref = rest.pop(0) if do_row else None
    lse_ref = rest.pop(0) if do_col else None
    w_ref = rest.pop(0) if emit_w else None
    p_ref = rest.pop(0) if emit_w else None
    fl_ref = rest.pop(0) if emit_w else None
    a_ref, b_ref = rest
    rows, cols = c_ref.shape
    groups = rows // GROUP
    chunks = cols // WIDTH

    if do_row:
        for j in range(chunks):
            cs = slice(j * WIDTH, (j + 1) * WIDTH)
            ev = every_ref[:, cs]
            top = jnp.max(ev, axis=0, keepdims=True)
            col_lse = top + jnp.log(jnp.sum(jnp.exp(ev - top), axis=0, keepdims=True))
            b_ref[:, cs] = (-shrink * EPS * col_lse) * (1.0 / EPS) + lb_ref[:, cs]
        rg = ROW_GROUP
        while rows % rg:
            rg //= 2

        def row_group(r, carry):
            rs = pl.ds(pl.multiple_of(r * rg, rg), rg)
            m = jnp.full((rg, WIDTH), -jnp.inf, jnp.float32)
            for j in range(chunks):
                cs = slice(j * WIDTH, (j + 1) * WIDTH)
                m = jnp.maximum(m, b_ref[:, cs] - c_ref[rs, cs])
            peak = jnp.max(m, axis=1, keepdims=True)
            s = jnp.zeros((rg, WIDTH), jnp.float32)
            for j in range(chunks):
                cs = slice(j * WIDTH, (j + 1) * WIDTH)
                s = s + jnp.exp(b_ref[:, cs] - c_ref[rs, cs] - peak)
            total = jnp.sum(s, axis=1, keepdims=True)
            pot = -shrink * EPS * (peak + jnp.log(total))
            f_ref[rs, :] = pot
            a_ref[rs, :] = jnp.broadcast_to(pot * (1.0 / EPS) + la_ref[rs, :], (rg, 128))
            if emit_w:
                for j in range(chunks):
                    cs = slice(j * WIDTH, (j + 1) * WIDTH)
                    e = jnp.exp(b_ref[:, cs] - c_ref[rs, cs] - peak)
                    w_ref[rs, cs] = (e / total).astype(w_ref.dtype)
                fl_ref[:, rs] = jnp.transpose(jnp.broadcast_to(pot, (rg, 128)))[0:1, :]
                p_ref[:, rs] = lax.dot_general(
                    handed_ref[...], w_ref[rs, :], (((1,), (1,)), ((), ())),
                    preferred_element_type=jnp.float32,
                )
            return carry
        lax.fori_loop(0, rows // rg, row_group, 0)
    else:
        a_ref[...] = jnp.broadcast_to(la_ref[...], a_ref.shape)

    if do_col:
        def col_chunk(j, carry):
            cs = pl.ds(pl.multiple_of(j * WIDTH, WIDTH), WIDTH)
            shifts = [jnp.tile(a_ref[r * GROUP:(r + 1) * GROUP, :], (1, WIDTH // 128))
                      for r in range(groups)]
            m = [jnp.full((GROUP, WIDTH), -jnp.inf, jnp.float32) for _ in range(2)]
            for r in range(groups):
                m[r % 2] = jnp.maximum(m[r % 2], shifts[r] - c_ref[r * GROUP:(r + 1) * GROUP, cs])
            peak = jnp.max(jnp.maximum(m[0], m[1]), axis=0, keepdims=True)
            s = [jnp.zeros((GROUP, WIDTH), jnp.float32) for _ in range(2)]
            for r in range(groups):
                s[r % 2] = s[r % 2] + jnp.exp(shifts[r] - c_ref[r * GROUP:(r + 1) * GROUP, cs] - peak)
            lse_ref[:, cs] = peak + jnp.log(jnp.sum(s[0] + s[1], axis=0, keepdims=True))
            return carry
        lax.fori_loop(0, chunks, col_chunk, 0)


def sweep(scaled_cost, every, log_b, log_a, shrink, do_row, do_col, emit_w, handed=None):
    rows, cols = scaled_cost.shape
    outs = []
    if do_row:
        outs.append(jax.ShapeDtypeStruct((rows, 1), jnp.float32))
    if do_col:
        outs.append(jax.ShapeDtypeStruct((1, cols), jnp.float32))
    if emit_w:
        outs.append(jax.ShapeDtypeStruct((rows, cols), jnp.bfloat16))
        outs.append(jax.ShapeDtypeStruct((handed.shape[0], rows), jnp.float32))
        outs.append(jax.ShapeDtypeStruct((1, rows), jnp.float32))
    passes = (2 if do_row else 0) + (2 if do_col else 0) + (1 if emit_w else 0)
    vmem = pl.BlockSpec(memory_space=pltpu.VMEM)
    return pl.pallas_call(
        functools.partial(sweep_kernel, do_row, do_col, emit_w, shrink),
        out_shape=tuple(outs),
        in_specs=[vmem] * (5 if emit_w else 4),
        out_specs=tuple([vmem] * len(outs)),
        scratch_shapes=[pltpu.VMEM((rows, 128), jnp.float32), pltpu.VMEM((1, cols), jnp.float32)],
        compiler_params=pltpu.CompilerParams(vmem_limit_bytes=24 * 1024 * 1024),
        cost_estimate=pl.CostEstimate(
            flops=4 * passes * rows * cols,
            transcendentals=passes * rows * cols // 2,
            bytes_accessed=4 * rows * cols + (2 * rows * cols if emit_w else 0),
        ),
    )(scaled_cost, every, log_b[None, :], log_a[:, None], *([handed] if emit_w else []))


def shifted(shard, axis, by):
    devices = lax.axis_size(axis)
    pairs = [(i, i + by) for i in range(devices) if 0 <= i + by < devices]
    return lax.ppermute(shard, axis, pairs)


def local(src_cells, final_cells, growth, live, final_fates):
    pair_count = lax.axis_size("pair")
    tgt_count = lax.axis_size("tgt")
    pair_rank = lax.axis_index("pair")
    src_rank = lax.axis_index("src")
    tgt_rank = lax.axis_index("tgt")
    shrink = LAM / (LAM + EPS)
    source_all = src_cells[0]
    dims = source_all.shape[0]
    src_width = source_all.shape[1]
    rows = src_width // tgt_count
    row_off = tgt_rank * rows
    is_last = pair_rank == pair_count - 1
    source_pos = lax.dynamic_slice_in_dim(source_all, row_off, rows, 1)
    group = lax.axis_size("src") * tgt_count
    src_count = lax.axis_size("src")
    arrived = shifted(source_all, "pair", -1)
    mine_next = lax.dynamic_slice_in_dim(arrived, row_off, rows, 1)
    fin_width = final_cells.shape[1]
    mine_final = lax.dynamic_slice_in_dim(final_cells, (src_rank * rows) % fin_width, rows, 1)
    piece = jnp.where(is_last, mine_final, mine_next)
    pieces = lax.all_gather(piece, ("src", "tgt"))
    per_fin = fin_width // rows
    final_order = [
        (b % per_fin) * tgt_count + b // per_fin if per_fin == src_count else b for b in range(group)
    ]
    if per_fin == src_count:
        final_pieces = pieces[jnp.array(final_order, dtype=jnp.int32)]
        pieces = jnp.where(is_last, final_pieces, pieces)
        target_pos = jnp.transpose(pieces, (1, 0, 2)).reshape(dims, group * rows)
    else:
        final_all = lax.all_gather(final_cells, "tgt", axis=1, tiled=True)
        target_pos = jnp.where(
            is_last, final_all, jnp.transpose(pieces, (1, 0, 2)).reshape(dims, group * rows)
        )
    cols = target_pos.shape[1]
    cross = lax.dot_general(
        source_pos,
        target_pos,
        (((0,), (0,)), ((), ())),
        precision=lax.Precision.HIGHEST,
        preferred_element_type=jnp.float32,
    )
    src_sq = jnp.sum(source_pos * source_pos, axis=0)
    tgt_sq = jnp.sum(target_pos * target_pos, axis=0)
    cost_tile = (src_sq[:, None] + tgt_sq[None, :] - 2.0 * cross) / (2.0 * dims)
    live_now = lax.dynamic_index_in_dim(live, pair_rank, keepdims=False)
    live_next = lax.dynamic_index_in_dim(live, pair_rank + 1, keepdims=False)
    row_index = src_rank * src_width + row_off + jnp.arange(rows, dtype=jnp.int32)
    col_index = jnp.arange(cols, dtype=jnp.int32)
    live_src = row_index < live_now
    live_tgt = col_index < live_next
    growth_rows = lax.dynamic_slice_in_dim(growth[0], row_off, rows, 0)
    log_mass_a = jnp.where(
        live_src, jnp.log(growth_rows) - jnp.log(live_now.astype(jnp.float32)), NEG
    )
    log_mass_b = jnp.where(
        live_tgt, -jnp.log(live_next.astype(jnp.float32)) * jnp.ones((cols,), jnp.float32), NEG
    )
    scaled_cost = cost_tile * (1.0 / EPS)
    final_handed = lax.all_gather(final_fates.astype(jnp.bfloat16), "tgt", axis=1, tiled=True)
    fates_count = final_handed.shape[0]
    fates_pad = -fates_count % 16
    handed_pad = jnp.concatenate(
        [final_handed, jnp.zeros((fates_pad, final_handed.shape[1]), jnp.bfloat16)], axis=0
    )
    (part_lse,) = sweep(scaled_cost, log_mass_b[None, :], log_mass_b, log_mass_a, shrink, False, True, False)
    for step_num in range(ITERS):
        every = lax.all_gather(part_lse[0], ("src", "tgt"))
        if step_num + 1 < ITERS:
            pot_col, part_lse = sweep(scaled_cost, every, log_mass_b, log_mass_a, shrink, True, True, False)
        else:
            pot_col, weights, first_pull, pot_lanes = sweep(
                scaled_cost, every, log_mass_b, log_mass_a, shrink, True, False, True, handed_pad
            )
    pot_src = pot_col.reshape(rows)
    handed = jnp.where(is_last, final_handed, jnp.zeros(final_handed.shape, jnp.bfloat16))
    fate_maps = jnp.zeros((final_fates.shape[0], rows), jnp.float32)
    for section_num in range(pair_count):
        active = pair_count - 1 - section_num
        if section_num == 0:
            pulled = first_pull[:fates_count]
        else:
            pulled = lax.dot_general(
                weights, handed, (((1,), (1,)), ((), ())), preferred_element_type=jnp.float32
            ).T
        pulled = jnp.where(live_src[None, :], pulled, 0.0)
        fate_maps = jnp.where(pair_rank == active, pulled, fate_maps)
        if section_num + 1 < pair_count:
            passed = shifted(pulled.astype(jnp.bfloat16), "pair", -1)
            fresh = lax.all_gather(passed, ("src", "tgt"), axis=1, tiled=True)
            handed = jnp.where(pair_rank == active - 1, fresh, handed)
    pot_all = lax.all_gather(pot_lanes.reshape(rows), "tgt", axis=0, tiled=True)
    return (fate_maps[None], pot_all[None])


def solution(mesh):
    placed = (P("pair", None, "src"), P(None, "tgt"), P("pair", "src"), P(), P(None, "tgt"))
    return jax.shard_map(
        local,
        mesh=mesh,
        in_specs=placed,
        out_specs=(P("pair", None, ("src", "tgt")), P("pair", "src")),
        check_vma=False,
    )
```

```python
import jax
import jax.numpy as jnp
from jax import lax
from jax.sharding import PartitionSpec as P
import functools
from jax.experimental import pallas as pl
from jax.experimental.pallas import tpu as pltpu

ITERS = 8


EPS = 0.1
LAM = 1.0
NEG = -1e30


GROUP = 16
ROW_GROUP = 128
WIDTH = 512


def sweep_kernel(do_row, do_col, emit_w, shrink, c_ref, every_ref, lb_ref, la_ref, *rest):
    rest = list(rest)
    handed_ref = rest.pop(0) if emit_w else None
    f_ref = rest.pop(0) if do_row else None
    lse_ref = rest.pop(0) if do_col else None
    w_ref = rest.pop(0) if emit_w else None
    p_ref = rest.pop(0) if emit_w else None
    fl_ref = rest.pop(0) if emit_w else None
    a_ref, b_ref = rest
    rows, cols = c_ref.shape
    groups = rows // GROUP
    chunks = cols // WIDTH

    if do_row:
        for j in range(chunks):
            cs = slice(j * WIDTH, (j + 1) * WIDTH)
            ev = every_ref[:, cs]
            top = jnp.max(ev, axis=0, keepdims=True)
            col_lse = top + jnp.log(jnp.sum(jnp.exp(ev - top), axis=0, keepdims=True))
            b_ref[:, cs] = (-shrink * EPS * col_lse) * (1.0 / EPS) + lb_ref[:, cs]
        rg = ROW_GROUP
        while rows % rg:
            rg //= 2

        def row_group(r, carry):
            rs = pl.ds(pl.multiple_of(r * rg, rg), rg)
            m = jnp.full((rg, WIDTH), -jnp.inf, jnp.float32)
            for j in range(chunks):
                cs = slice(j * WIDTH, (j + 1) * WIDTH)
                m = jnp.maximum(m, b_ref[:, cs] - c_ref[rs, cs])
            peak = jnp.max(m, axis=1, keepdims=True)
            s = jnp.zeros((rg, WIDTH), jnp.float32)
            for j in range(chunks):
                cs = slice(j * WIDTH, (j + 1) * WIDTH)
                s = s + jnp.exp(b_ref[:, cs] - c_ref[rs, cs] - peak)
            total = jnp.sum(s, axis=1, keepdims=True)
            pot = -shrink * EPS * (peak + jnp.log(total))
            f_ref[rs, :] = pot
            a_ref[rs, :] = jnp.broadcast_to(pot * (1.0 / EPS) + la_ref[rs, :], (rg, 128))
            if emit_w:
                for j in range(chunks):
                    cs = slice(j * WIDTH, (j + 1) * WIDTH)
                    e = jnp.exp(b_ref[:, cs] - c_ref[rs, cs] - peak)
                    w_ref[rs, cs] = (e / total).astype(w_ref.dtype)
                fl_ref[:, rs] = jnp.transpose(jnp.broadcast_to(pot, (rg, 128)))[0:1, :]
                p_ref[:, rs] = lax.dot_general(
                    handed_ref[...], w_ref[rs, :], (((1,), (1,)), ((), ())),
                    preferred_element_type=jnp.float32,
                )
            return carry
        lax.fori_loop(0, rows // rg, row_group, 0)
    else:
        a_ref[...] = jnp.broadcast_to(la_ref[...], a_ref.shape)

    if do_col:
        def col_chunk(j, carry):
            cs = pl.ds(pl.multiple_of(j * WIDTH, WIDTH), WIDTH)
            shifts = [jnp.tile(a_ref[r * GROUP:(r + 1) * GROUP, :], (1, WIDTH // 128))
                      for r in range(groups)]
            m = [jnp.full((GROUP, WIDTH), -jnp.inf, jnp.float32) for _ in range(2)]
            for r in range(groups):
                m[r % 2] = jnp.maximum(m[r % 2], shifts[r] - c_ref[r * GROUP:(r + 1) * GROUP, cs])
            peak = jnp.max(jnp.maximum(m[0], m[1]), axis=0, keepdims=True)
            s = [jnp.zeros((GROUP, WIDTH), jnp.float32) for _ in range(2)]
            for r in range(groups):
                s[r % 2] = s[r % 2] + jnp.exp(shifts[r] - c_ref[r * GROUP:(r + 1) * GROUP, cs] - peak)
            lse_ref[:, cs] = peak + jnp.log(jnp.sum(s[0] + s[1], axis=0, keepdims=True))
            return carry
        lax.fori_loop(0, chunks, col_chunk, 0)


def sweep(scaled_cost, every, log_b, log_a, shrink, do_row, do_col, emit_w, handed=None):
    rows, cols = scaled_cost.shape
    outs = []
    if do_row:
        outs.append(jax.ShapeDtypeStruct((rows, 1), jnp.float32))
    if do_col:
        outs.append(jax.ShapeDtypeStruct((1, cols), jnp.float32))
    if emit_w:
        outs.append(jax.ShapeDtypeStruct((rows, cols), jnp.bfloat16))
        outs.append(jax.ShapeDtypeStruct((handed.shape[0], rows), jnp.float32))
        outs.append(jax.ShapeDtypeStruct((1, rows), jnp.float32))
    passes = (2 if do_row else 0) + (2 if do_col else 0) + (1 if emit_w else 0)
    vmem = pl.BlockSpec(memory_space=pltpu.VMEM)
    return pl.pallas_call(
        functools.partial(sweep_kernel, do_row, do_col, emit_w, shrink),
        out_shape=tuple(outs),
        in_specs=[vmem] * (5 if emit_w else 4),
        out_specs=tuple([vmem] * len(outs)),
        scratch_shapes=[pltpu.VMEM((rows, 128), jnp.float32), pltpu.VMEM((1, cols), jnp.float32)],
        compiler_params=pltpu.CompilerParams(vmem_limit_bytes=24 * 1024 * 1024),
        cost_estimate=pl.CostEstimate(
            flops=4 * passes * rows * cols,
            transcendentals=passes * rows * cols // 2,
            bytes_accessed=4 * rows * cols + (2 * rows * cols if emit_w else 0),
        ),
    )(scaled_cost, every, log_b[None, :], log_a[:, None], *([handed] if emit_w else []))


def pull_kernel(handed_ref, w_ref, out_ref):
    out_ref[...] = lax.dot_general(
        handed_ref[...], w_ref[...], (((1,), (1,)), ((), ())), preferred_element_type=jnp.float32
    )


def pull(handed, weights):
    vmem = pl.BlockSpec(memory_space=pltpu.VMEM)
    fates, cols = handed.shape
    rows = weights.shape[0]
    return pl.pallas_call(
        pull_kernel,
        out_shape=jax.ShapeDtypeStruct((fates, rows), jnp.float32),
        in_specs=[vmem, vmem],
        out_specs=vmem,
        compiler_params=pltpu.CompilerParams(vmem_limit_bytes=8 * 1024 * 1024),
        cost_estimate=pl.CostEstimate(
            flops=2 * fates * rows * cols, transcendentals=0, bytes_accessed=2 * (fates + rows) * cols
        ),
    )(handed, weights)


def shifted(shard, axis, by):
    devices = lax.axis_size(axis)
    pairs = [(i, i + by) for i in range(devices) if 0 <= i + by < devices]
    return lax.ppermute(shard, axis, pairs)


def local(src_cells, final_cells, growth, live, final_fates):
    pair_count = lax.axis_size("pair")
    tgt_count = lax.axis_size("tgt")
    pair_rank = lax.axis_index("pair")
    src_rank = lax.axis_index("src")
    tgt_rank = lax.axis_index("tgt")
    shrink = LAM / (LAM + EPS)
    source_all = src_cells[0]
    dims = source_all.shape[0]
    src_width = source_all.shape[1]
    rows = src_width // tgt_count
    row_off = tgt_rank * rows
    is_last = pair_rank == pair_count - 1
    source_pos = lax.dynamic_slice_in_dim(source_all, row_off, rows, 1)
    group = lax.axis_size("src") * tgt_count
    src_count = lax.axis_size("src")
    arrived = shifted(source_all, "pair", -1)
    mine_next = lax.dynamic_slice_in_dim(arrived, row_off, rows, 1)
    fin_width = final_cells.shape[1]
    mine_final = lax.dynamic_slice_in_dim(final_cells, (src_rank * rows) % fin_width, rows, 1)
    piece = jnp.where(is_last, mine_final, mine_next)
    pieces = lax.all_gather(piece, ("src", "tgt"))
    per_fin = fin_width // rows
    final_order = [
        (b % per_fin) * tgt_count + b // per_fin if per_fin == src_count else b for b in range(group)
    ]
    if per_fin == src_count:
        final_pieces = pieces[jnp.array(final_order, dtype=jnp.int32)]
        pieces = jnp.where(is_last, final_pieces, pieces)
        target_pos = jnp.transpose(pieces, (1, 0, 2)).reshape(dims, group * rows)
    else:
        final_all = lax.all_gather(final_cells, "tgt", axis=1, tiled=True)
        target_pos = jnp.where(
            is_last, final_all, jnp.transpose(pieces, (1, 0, 2)).reshape(dims, group * rows)
        )
    cols = target_pos.shape[1]
    cross = lax.dot_general(
        source_pos,
        target_pos,
        (((0,), (0,)), ((), ())),
        precision=lax.Precision.HIGHEST,
        preferred_element_type=jnp.float32,
    )
    src_sq = jnp.sum(source_pos * source_pos, axis=0)
    tgt_sq = jnp.sum(target_pos * target_pos, axis=0)
    cost_tile = (src_sq[:, None] + tgt_sq[None, :] - 2.0 * cross) / (2.0 * dims)
    live_now = lax.dynamic_index_in_dim(live, pair_rank, keepdims=False)
    live_next = lax.dynamic_index_in_dim(live, pair_rank + 1, keepdims=False)
    row_index = src_rank * src_width + row_off + jnp.arange(rows, dtype=jnp.int32)
    col_index = jnp.arange(cols, dtype=jnp.int32)
    live_src = row_index < live_now
    live_tgt = col_index < live_next
    growth_rows = lax.dynamic_slice_in_dim(growth[0], row_off, rows, 0)
    log_mass_a = jnp.where(
        live_src, jnp.log(growth_rows) - jnp.log(live_now.astype(jnp.float32)), NEG
    )
    log_mass_b = jnp.where(
        live_tgt, -jnp.log(live_next.astype(jnp.float32)) * jnp.ones((cols,), jnp.float32), NEG
    )
    scaled_cost = cost_tile * (1.0 / EPS)
    final_handed = lax.all_gather(final_fates.astype(jnp.bfloat16), "tgt", axis=1, tiled=True)
    fates_count = final_handed.shape[0]
    fates_pad = -fates_count % 16
    handed_pad = jnp.concatenate(
        [final_handed, jnp.zeros((fates_pad, final_handed.shape[1]), jnp.bfloat16)], axis=0
    )
    (part_lse,) = sweep(scaled_cost, log_mass_b[None, :], log_mass_b, log_mass_a, shrink, False, True, False)
    for step_num in range(ITERS):
        every = lax.all_gather(part_lse[0], ("src", "tgt"))
        if step_num + 1 < ITERS:
            pot_col, part_lse = sweep(scaled_cost, every, log_mass_b, log_mass_a, shrink, True, True, False)
        else:
            pot_col, weights, first_pull, pot_lanes = sweep(
                scaled_cost, every, log_mass_b, log_mass_a, shrink, True, False, True, handed_pad
            )
    pot_src = pot_col.reshape(rows)
    handed = jnp.where(is_last, final_handed, jnp.zeros(final_handed.shape, jnp.bfloat16))
    fate_maps = jnp.zeros((final_fates.shape[0], rows), jnp.float32)
    for section_num in range(pair_count):
        active = pair_count - 1 - section_num
        if section_num == 0:
            pulled = first_pull[:fates_count]
        else:
            pulled = pull(handed, weights)
        pulled = jnp.where(live_src[None, :], pulled, 0.0)
        fate_maps = jnp.where(pair_rank == active, pulled, fate_maps)
        if section_num + 1 < pair_count:
            passed = shifted(pulled.astype(jnp.bfloat16), "pair", -1)
            fresh = lax.all_gather(passed, ("src", "tgt"), axis=1, tiled=True)
            handed = jnp.where(pair_rank == active - 1, fresh, handed)
    pot_all = lax.all_gather(pot_lanes.reshape(rows), "tgt", axis=0, tiled=True)
    return (fate_maps[None], pot_all[None])


def solution(mesh):
    placed = (P("pair", None, "src"), P(None, "tgt"), P("pair", "src"), P(), P(None, "tgt"))
    return jax.shard_map(
        local,
        mesh=mesh,
        in_specs=placed,
        out_specs=(P("pair", None, ("src", "tgt")), P("pair", "src")),
        check_vma=False,
    )
```

```python
import jax
import jax.numpy as jnp
from jax import lax
from jax.sharding import PartitionSpec as P
import functools
from jax.experimental import pallas as pl
from jax.experimental.pallas import tpu as pltpu

ITERS = 8


EPS = 0.1
LAM = 1.0
NEG = -1e30


GROUP = 32
ROW_GROUP = 128
WIDTH = 512


def sweep_kernel(do_row, do_col, emit_w, shrink, c_ref, every_ref, lb_ref, la_ref, *rest):
    rest = list(rest)
    handed_ref = rest.pop(0) if emit_w else None
    f_ref = rest.pop(0) if do_row else None
    lse_ref = rest.pop(0) if do_col else None
    w_ref = rest.pop(0) if emit_w else None
    p_ref = rest.pop(0) if emit_w else None
    fl_ref = rest.pop(0) if emit_w else None
    a_ref, b_ref = rest
    rows, cols = c_ref.shape
    groups = rows // GROUP
    chunks = cols // WIDTH

    if do_row:
        for j in range(chunks):
            cs = slice(j * WIDTH, (j + 1) * WIDTH)
            ev = every_ref[:, cs]
            top = jnp.max(ev, axis=0, keepdims=True)
            col_lse = top + jnp.log(jnp.sum(jnp.exp(ev - top), axis=0, keepdims=True))
            b_ref[:, cs] = (-shrink * EPS * col_lse) * (1.0 / EPS) + lb_ref[:, cs]
        rg = ROW_GROUP
        while rows % rg:
            rg //= 2

        def row_group(r, carry):
            rs = pl.ds(pl.multiple_of(r * rg, rg), rg)
            m = jnp.full((rg, WIDTH), -jnp.inf, jnp.float32)
            for j in range(chunks):
                cs = slice(j * WIDTH, (j + 1) * WIDTH)
                m = jnp.maximum(m, b_ref[:, cs] - c_ref[rs, cs])
            peak = jnp.max(m, axis=1, keepdims=True)
            s = jnp.zeros((rg, WIDTH), jnp.float32)
            for j in range(chunks):
                cs = slice(j * WIDTH, (j + 1) * WIDTH)
                s = s + jnp.exp(b_ref[:, cs] - c_ref[rs, cs] - peak)
            total = jnp.sum(s, axis=1, keepdims=True)
            pot = -shrink * EPS * (peak + jnp.log(total))
            f_ref[rs, :] = pot
            a_ref[rs, :] = jnp.broadcast_to(pot * (1.0 / EPS) + la_ref[rs, :], (rg, 128))
            if emit_w:
                for j in range(chunks):
                    cs = slice(j * WIDTH, (j + 1) * WIDTH)
                    e = jnp.exp(b_ref[:, cs] - c_ref[rs, cs] - peak)
                    w_ref[rs, cs] = (e / total).astype(w_ref.dtype)
                fl_ref[:, rs] = jnp.transpose(jnp.broadcast_to(pot, (rg, 128)))[0:1, :]
                p_ref[:, rs] = lax.dot_general(
                    handed_ref[...], w_ref[rs, :], (((1,), (1,)), ((), ())),
                    preferred_element_type=jnp.float32,
                )
            return carry
        lax.fori_loop(0, rows // rg, row_group, 0)
    else:
        a_ref[...] = jnp.broadcast_to(la_ref[...], a_ref.shape)

    if do_col:
        def col_chunk(j, carry):
            cs = pl.ds(pl.multiple_of(j * WIDTH, WIDTH), WIDTH)
            shifts = [jnp.tile(a_ref[r * GROUP:(r + 1) * GROUP, :], (1, WIDTH // 128))
                      for r in range(groups)]
            m = [jnp.full((GROUP, WIDTH), -jnp.inf, jnp.float32) for _ in range(2)]
            for r in range(groups):
                m[r % 2] = jnp.maximum(m[r % 2], shifts[r] - c_ref[r * GROUP:(r + 1) * GROUP, cs])
            peak = jnp.max(jnp.maximum(m[0], m[1]), axis=0, keepdims=True)
            s = [jnp.zeros((GROUP, WIDTH), jnp.float32) for _ in range(2)]
            for r in range(groups):
                s[r % 2] = s[r % 2] + jnp.exp(shifts[r] - c_ref[r * GROUP:(r + 1) * GROUP, cs] - peak)
            lse_ref[:, cs] = peak + jnp.log(jnp.sum(s[0] + s[1], axis=0, keepdims=True))
            return carry
        lax.fori_loop(0, chunks, col_chunk, 0)


def sweep(scaled_cost, every, log_b, log_a, shrink, do_row, do_col, emit_w, handed=None):
    rows, cols = scaled_cost.shape
    outs = []
    if do_row:
        outs.append(jax.ShapeDtypeStruct((rows, 1), jnp.float32))
    if do_col:
        outs.append(jax.ShapeDtypeStruct((1, cols), jnp.float32))
    if emit_w:
        outs.append(jax.ShapeDtypeStruct((rows, cols), jnp.bfloat16))
        outs.append(jax.ShapeDtypeStruct((handed.shape[0], rows), jnp.float32))
        outs.append(jax.ShapeDtypeStruct((1, rows), jnp.float32))
    passes = (2 if do_row else 0) + (2 if do_col else 0) + (1 if emit_w else 0)
    vmem = pl.BlockSpec(memory_space=pltpu.VMEM)
    return pl.pallas_call(
        functools.partial(sweep_kernel, do_row, do_col, emit_w, shrink),
        out_shape=tuple(outs),
        in_specs=[vmem] * (5 if emit_w else 4),
        out_specs=tuple([vmem] * len(outs)),
        scratch_shapes=[pltpu.VMEM((rows, 128), jnp.float32), pltpu.VMEM((1, cols), jnp.float32)],
        compiler_params=pltpu.CompilerParams(vmem_limit_bytes=24 * 1024 * 1024),
        cost_estimate=pl.CostEstimate(
            flops=4 * passes * rows * cols,
            transcendentals=passes * rows * cols // 2,
            bytes_accessed=4 * rows * cols + (2 * rows * cols if emit_w else 0),
        ),
    )(scaled_cost, every, log_b[None, :], log_a[:, None], *([handed] if emit_w else []))


def shifted(shard, axis, by):
    devices = lax.axis_size(axis)
    pairs = [(i, i + by) for i in range(devices) if 0 <= i + by < devices]
    return lax.ppermute(shard, axis, pairs)


def local(src_cells, final_cells, growth, live, final_fates):
    pair_count = lax.axis_size("pair")
    tgt_count = lax.axis_size("tgt")
    pair_rank = lax.axis_index("pair")
    src_rank = lax.axis_index("src")
    tgt_rank = lax.axis_index("tgt")
    shrink = LAM / (LAM + EPS)
    source_all = src_cells[0]
    dims = source_all.shape[0]
    src_width = source_all.shape[1]
    rows = src_width // tgt_count
    row_off = tgt_rank * rows
    is_last = pair_rank == pair_count - 1
    source_pos = lax.dynamic_slice_in_dim(source_all, row_off, rows, 1)
    group = lax.axis_size("src") * tgt_count
    src_count = lax.axis_size("src")
    arrived = shifted(source_all, "pair", -1)
    mine_next = lax.dynamic_slice_in_dim(arrived, row_off, rows, 1)
    fin_width = final_cells.shape[1]
    mine_final = lax.dynamic_slice_in_dim(final_cells, (src_rank * rows) % fin_width, rows, 1)
    piece = jnp.where(is_last, mine_final, mine_next)
    pieces = lax.all_gather(piece, ("src", "tgt"))
    per_fin = fin_width // rows
    final_order = [
        (b % per_fin) * tgt_count + b // per_fin if per_fin == src_count else b for b in range(group)
    ]
    if per_fin == src_count:
        final_pieces = pieces[jnp.array(final_order, dtype=jnp.int32)]
        pieces = jnp.where(is_last, final_pieces, pieces)
        target_pos = jnp.transpose(pieces, (1, 0, 2)).reshape(dims, group * rows)
    else:
        final_all = lax.all_gather(final_cells, "tgt", axis=1, tiled=True)
        target_pos = jnp.where(
            is_last, final_all, jnp.transpose(pieces, (1, 0, 2)).reshape(dims, group * rows)
        )
    cols = target_pos.shape[1]
    cross = lax.dot_general(
        source_pos,
        target_pos,
        (((0,), (0,)), ((), ())),
        precision=lax.Precision.HIGHEST,
        preferred_element_type=jnp.float32,
    )
    src_sq = jnp.sum(source_pos * source_pos, axis=0)
    tgt_sq = jnp.sum(target_pos * target_pos, axis=0)
    cost_tile = (src_sq[:, None] + tgt_sq[None, :] - 2.0 * cross) / (2.0 * dims)
    live_now = lax.dynamic_index_in_dim(live, pair_rank, keepdims=False)
    live_next = lax.dynamic_index_in_dim(live, pair_rank + 1, keepdims=False)
    row_index = src_rank * src_width + row_off + jnp.arange(rows, dtype=jnp.int32)
    col_index = jnp.arange(cols, dtype=jnp.int32)
    live_src = row_index < live_now
    live_tgt = col_index < live_next
    growth_rows = lax.dynamic_slice_in_dim(growth[0], row_off, rows, 0)
    log_mass_a = jnp.where(
        live_src, jnp.log(growth_rows) - jnp.log(live_now.astype(jnp.float32)), NEG
    )
    log_mass_b = jnp.where(
        live_tgt, -jnp.log(live_next.astype(jnp.float32)) * jnp.ones((cols,), jnp.float32), NEG
    )
    scaled_cost = cost_tile * (1.0 / EPS)
    final_handed = lax.all_gather(final_fates.astype(jnp.bfloat16), "tgt", axis=1, tiled=True)
    fates_count = final_handed.shape[0]
    fates_pad = -fates_count % 16
    handed_pad = jnp.concatenate(
        [final_handed, jnp.zeros((fates_pad, final_handed.shape[1]), jnp.bfloat16)], axis=0
    )
    (part_lse,) = sweep(scaled_cost, log_mass_b[None, :], log_mass_b, log_mass_a, shrink, False, True, False)
    for step_num in range(ITERS):
        every = lax.all_gather(part_lse[0], ("src", "tgt"))
        if step_num + 1 < ITERS:
            pot_col, part_lse = sweep(scaled_cost, every, log_mass_b, log_mass_a, shrink, True, True, False)
        else:
            pot_col, weights, first_pull, pot_lanes = sweep(
                scaled_cost, every, log_mass_b, log_mass_a, shrink, True, False, True, handed_pad
            )
    pot_src = pot_col.reshape(rows)
    handed = jnp.where(is_last, final_handed, jnp.zeros(final_handed.shape, jnp.bfloat16))
    fate_maps = jnp.zeros((final_fates.shape[0], rows), jnp.float32)
    for section_num in range(pair_count):
        active = pair_count - 1 - section_num
        if section_num == 0:
            pulled = first_pull[:fates_count]
        else:
            pulled = lax.dot_general(
                weights, handed, (((1,), (1,)), ((), ())), preferred_element_type=jnp.float32
            ).T
        pulled = jnp.where(live_src[None, :], pulled, 0.0)
        fate_maps = jnp.where(pair_rank == active, pulled, fate_maps)
        if section_num + 1 < pair_count:
            passed = shifted(pulled.astype(jnp.bfloat16), "pair", -1)
            fresh = lax.all_gather(passed, ("src", "tgt"), axis=1, tiled=True)
            handed = jnp.where(pair_rank == active - 1, fresh, handed)
    pot_all = lax.all_gather(pot_lanes.reshape(rows), "tgt", axis=0, tiled=True)
    return (fate_maps[None], pot_all[None])


def solution(mesh):
    placed = (P("pair", None, "src"), P(None, "tgt"), P("pair", "src"), P(), P(None, "tgt"))
    return jax.shard_map(
        local,
        mesh=mesh,
        in_specs=placed,
        out_specs=(P("pair", None, ("src", "tgt")), P("pair", "src")),
        check_vma=False,
    )
```

```python
import jax
import jax.numpy as jnp
from jax import lax
from jax.sharding import PartitionSpec as P
import functools
from jax.experimental import pallas as pl
from jax.experimental.pallas import tpu as pltpu

ITERS = 8


EPS = 0.1
LAM = 1.0
NEG = -1e30


GROUP = 32
ROW_GROUP = 128
WIDTH = 512


def sweep_kernel(do_row, do_col, emit_w, shrink, c_ref, every_ref, lb_ref, la_ref, *rest):
    rest = list(rest)
    handed_ref = rest.pop(0) if emit_w else None
    f_ref = rest.pop(0) if do_row else None
    lse_ref = rest.pop(0) if do_col else None
    w_ref = rest.pop(0) if emit_w else None
    p_ref = rest.pop(0) if emit_w else None
    fl_ref = rest.pop(0) if emit_w else None
    a_ref, b_ref = rest
    rows, cols = c_ref.shape
    groups = rows // GROUP
    chunks = cols // WIDTH

    if do_row:
        for j in range(chunks):
            cs = slice(j * WIDTH, (j + 1) * WIDTH)
            ev = every_ref[:, cs]
            top = jnp.max(ev, axis=0, keepdims=True)
            col_lse = top + jnp.log(jnp.sum(jnp.exp(ev - top), axis=0, keepdims=True))
            b_ref[:, cs] = (-shrink * EPS * col_lse) * (1.0 / EPS) + lb_ref[:, cs]
        rg = ROW_GROUP
        while rows % rg:
            rg //= 2

        def row_group(r, carry):
            rs = pl.ds(pl.multiple_of(r * rg, rg), rg)
            m = jnp.full((rg, WIDTH), -jnp.inf, jnp.float32)
            for j in range(chunks):
                cs = slice(j * WIDTH, (j + 1) * WIDTH)
                m = jnp.maximum(m, b_ref[:, cs] - c_ref[rs, cs])
            peak = jnp.max(m, axis=1, keepdims=True)
            s = jnp.zeros((rg, WIDTH), jnp.float32)
            for j in range(chunks):
                cs = slice(j * WIDTH, (j + 1) * WIDTH)
                s = s + jnp.exp(b_ref[:, cs] - c_ref[rs, cs] - peak)
            total = jnp.sum(s, axis=1, keepdims=True)
            pot = -shrink * EPS * (peak + jnp.log(total))
            f_ref[rs, :] = pot
            a_ref[rs, :] = jnp.broadcast_to(pot * (1.0 / EPS) + la_ref[rs, :], (rg, 128))
            if emit_w:
                for j in range(chunks):
                    cs = slice(j * WIDTH, (j + 1) * WIDTH)
                    e = jnp.exp(b_ref[:, cs] - c_ref[rs, cs] - peak)
                    w_ref[rs, cs] = (e / total).astype(w_ref.dtype)
                fl_ref[:, rs] = jnp.transpose(jnp.broadcast_to(pot, (rg, 128)))[0:1, :]
                p_ref[:, rs] = lax.dot_general(
                    handed_ref[...], w_ref[rs, :], (((1,), (1,)), ((), ())),
                    preferred_element_type=jnp.float32,
                )
            return carry
        lax.fori_loop(0, rows // rg, row_group, 0)
    else:
        a_ref[...] = jnp.broadcast_to(la_ref[...], a_ref.shape)

    if do_col:
        def col_chunk(j, carry):
            cs = pl.ds(pl.multiple_of(j * WIDTH, WIDTH), WIDTH)
            shifts = [jnp.tile(a_ref[r * GROUP:(r + 1) * GROUP, :], (1, WIDTH // 128))
                      for r in range(groups)]
            m = [jnp.full((GROUP, WIDTH), -jnp.inf, jnp.float32) for _ in range(2)]
            for r in range(groups):
                m[r % 2] = jnp.maximum(m[r % 2], shifts[r] - c_ref[r * GROUP:(r + 1) * GROUP, cs])
            peak = jnp.max(jnp.maximum(m[0], m[1]), axis=0, keepdims=True)
            s = [jnp.zeros((GROUP, WIDTH), jnp.float32) for _ in range(2)]
            for r in range(groups):
                s[r % 2] = s[r % 2] + jnp.exp(shifts[r] - c_ref[r * GROUP:(r + 1) * GROUP, cs] - peak)
            lse_ref[:, cs] = peak + jnp.log(jnp.sum(s[0] + s[1], axis=0, keepdims=True))
            return carry
        lax.fori_loop(0, chunks, col_chunk, 0)


def sweep(scaled_cost, every, log_b, log_a, shrink, do_row, do_col, emit_w, handed=None):
    rows, cols = scaled_cost.shape
    outs = []
    if do_row:
        outs.append(jax.ShapeDtypeStruct((rows, 1), jnp.float32))
    if do_col:
        outs.append(jax.ShapeDtypeStruct((1, cols), jnp.float32))
    if emit_w:
        outs.append(jax.ShapeDtypeStruct((rows, cols), jnp.bfloat16))
        outs.append(jax.ShapeDtypeStruct((handed.shape[0], rows), jnp.float32))
        outs.append(jax.ShapeDtypeStruct((1, rows), jnp.float32))
    passes = (2 if do_row else 0) + (2 if do_col else 0) + (1 if emit_w else 0)
    vmem = pl.BlockSpec(memory_space=pltpu.VMEM)
    return pl.pallas_call(
        functools.partial(sweep_kernel, do_row, do_col, emit_w, shrink),
        out_shape=tuple(outs),
        in_specs=[vmem] * (5 if emit_w else 4),
        out_specs=tuple([vmem] * len(outs)),
        scratch_shapes=[pltpu.VMEM((rows, 128), jnp.float32), pltpu.VMEM((1, cols), jnp.float32)],
        compiler_params=pltpu.CompilerParams(vmem_limit_bytes=24 * 1024 * 1024),
        cost_estimate=pl.CostEstimate(
            flops=4 * passes * rows * cols,
            transcendentals=passes * rows * cols // 2,
            bytes_accessed=4 * rows * cols + (2 * rows * cols if emit_w else 0),
        ),
    )(scaled_cost, every, log_b[None, :], log_a[:, None], *([handed] if emit_w else []))


def shifted(shard, axis, by):
    devices = lax.axis_size(axis)
    pairs = [(i, i + by) for i in range(devices) if 0 <= i + by < devices]
    return lax.ppermute(shard, axis, pairs)


def local(src_cells, final_cells, growth, live, final_fates):
    pair_count = lax.axis_size("pair")
    tgt_count = lax.axis_size("tgt")
    pair_rank = lax.axis_index("pair")
    src_rank = lax.axis_index("src")
    tgt_rank = lax.axis_index("tgt")
    shrink = LAM / (LAM + EPS)
    source_all = src_cells[0]
    dims = source_all.shape[0]
    src_width = source_all.shape[1]
    rows = src_width // tgt_count
    row_off = tgt_rank * rows
    is_last = pair_rank == pair_count - 1
    source_pos = lax.dynamic_slice_in_dim(source_all, row_off, rows, 1)
    group = lax.axis_size("src") * tgt_count
    src_count = lax.axis_size("src")
    arrived = shifted(source_all, "pair", -1)
    mine_next = lax.dynamic_slice_in_dim(arrived, row_off, rows, 1)
    fin_width = final_cells.shape[1]
    mine_final = lax.dynamic_slice_in_dim(final_cells, (src_rank * rows) % fin_width, rows, 1)
    piece = jnp.where(is_last, mine_final, mine_next)
    pieces = lax.all_gather(piece, ("src", "tgt"))
    per_fin = fin_width // rows
    final_order = [
        (b % per_fin) * tgt_count + b // per_fin if per_fin == src_count else b for b in range(group)
    ]
    if per_fin == src_count:
        final_pieces = pieces[jnp.array(final_order, dtype=jnp.int32)]
        pieces = jnp.where(is_last, final_pieces, pieces)
        target_pos = jnp.transpose(pieces, (1, 0, 2)).reshape(dims, group * rows)
    else:
        final_all = lax.all_gather(final_cells, "tgt", axis=1, tiled=True)
        target_pos = jnp.where(
            is_last, final_all, jnp.transpose(pieces, (1, 0, 2)).reshape(dims, group * rows)
        )
    cols = target_pos.shape[1]
    cross = lax.dot_general(
        source_pos,
        target_pos,
        (((0,), (0,)), ((), ())),
        precision=lax.Precision.HIGHEST,
        preferred_element_type=jnp.float32,
    )
    src_sq = jnp.sum(source_pos * source_pos, axis=0)
    tgt_sq = jnp.sum(target_pos * target_pos, axis=0)
    cost_tile = (src_sq[:, None] + tgt_sq[None, :] - 2.0 * cross) / (2.0 * dims)
    live_now = lax.dynamic_index_in_dim(live, pair_rank, keepdims=False)
    live_next = lax.dynamic_index_in_dim(live, pair_rank + 1, keepdims=False)
    row_index = src_rank * src_width + row_off + jnp.arange(rows, dtype=jnp.int32)
    col_index = jnp.arange(cols, dtype=jnp.int32)
    live_src = row_index < live_now
    live_tgt = col_index < live_next
    growth_rows = lax.dynamic_slice_in_dim(growth[0], row_off, rows, 0)
    log_mass_a = jnp.where(
        live_src, jnp.log(growth_rows) - jnp.log(live_now.astype(jnp.float32)), NEG
    )
    log_mass_b = jnp.where(
        live_tgt, -jnp.log(live_next.astype(jnp.float32)) * jnp.ones((cols,), jnp.float32), NEG
    )
    scaled_cost = cost_tile * (1.0 / EPS)
    fin_fates = final_fates.astype(jnp.bfloat16)
    if tgt_count <= 4:
        got = [fin_fates] + [
            lax.ppermute(fin_fates, "tgt", [(i, (i + k) % tgt_count) for i in range(tgt_count)])
            for k in range(1, tgt_count)
        ]
        order = (tgt_rank - jnp.arange(tgt_count, dtype=jnp.int32)) % tgt_count
        got = jnp.take(jnp.stack(got), order, axis=0)
        final_handed = jnp.transpose(got, (1, 0, 2)).reshape(fin_fates.shape[0], tgt_count * fin_width)
    else:
        final_handed = lax.all_gather(fin_fates, "tgt", axis=1, tiled=True)
    fates_count = final_handed.shape[0]
    fates_pad = -fates_count % 16
    handed_pad = jnp.concatenate(
        [final_handed, jnp.zeros((fates_pad, final_handed.shape[1]), jnp.bfloat16)], axis=0
    )
    (part_lse,) = sweep(scaled_cost, log_mass_b[None, :], log_mass_b, log_mass_a, shrink, False, True, False)
    for step_num in range(ITERS):
        every = lax.all_gather(part_lse[0], ("src", "tgt"))
        if step_num + 1 < ITERS:
            pot_col, part_lse = sweep(scaled_cost, every, log_mass_b, log_mass_a, shrink, True, True, False)
        else:
            pot_col, weights, first_pull, pot_lanes = sweep(
                scaled_cost, every, log_mass_b, log_mass_a, shrink, True, False, True, handed_pad
            )
    pot_src = pot_col.reshape(rows)
    handed = jnp.where(is_last, final_handed, jnp.zeros(final_handed.shape, jnp.bfloat16))
    fate_maps = jnp.zeros((final_fates.shape[0], rows), jnp.float32)
    for section_num in range(pair_count):
        active = pair_count - 1 - section_num
        if section_num == 0:
            pulled = first_pull[:fates_count]
        else:
            pulled = lax.dot_general(
                weights, handed, (((1,), (1,)), ((), ())), preferred_element_type=jnp.float32
            ).T
        pulled = jnp.where(live_src[None, :], pulled, 0.0)
        fate_maps = jnp.where(pair_rank == active, pulled, fate_maps)
        if section_num + 1 < pair_count:
            passed = shifted(pulled.astype(jnp.bfloat16), "pair", -1)
            fresh = lax.all_gather(passed, ("src", "tgt"), axis=1, tiled=True)
            handed = jnp.where(pair_rank == active - 1, fresh, handed)
    pot_all = lax.all_gather(pot_lanes.reshape(rows), "tgt", axis=0, tiled=True)
    return (fate_maps[None], pot_all[None])


def solution(mesh):
    placed = (P("pair", None, "src"), P(None, "tgt"), P("pair", "src"), P(), P(None, "tgt"))
    return jax.shard_map(
        local,
        mesh=mesh,
        in_specs=placed,
        out_specs=(P("pair", None, ("src", "tgt")), P("pair", "src")),
        check_vma=False,
    )
```

```python
import jax
import jax.numpy as jnp
from jax import lax
from jax.sharding import PartitionSpec as P
import functools
from jax.experimental import pallas as pl
from jax.experimental.pallas import tpu as pltpu

ITERS = 8


EPS = 0.1
LAM = 1.0
NEG = -1e30


GROUP = 32
ROW_GROUP = 128
WIDTH = 512


def sweep_kernel(do_row, do_col, emit_w, shrink, c_ref, every_ref, lb_ref, la_ref, *rest):
    rest = list(rest)
    handed_ref = rest.pop(0) if emit_w else None
    f_ref = rest.pop(0) if do_row else None
    lse_ref = rest.pop(0) if do_col else None
    w_ref = rest.pop(0) if emit_w else None
    p_ref = rest.pop(0) if emit_w else None
    fl_ref = rest.pop(0) if emit_w else None
    a_ref, b_ref = rest
    rows, cols = c_ref.shape
    groups = rows // GROUP
    chunks = cols // WIDTH

    if do_row:
        for j in range(chunks):
            cs = slice(j * WIDTH, (j + 1) * WIDTH)
            ev = every_ref[:, cs]
            top = jnp.max(ev, axis=0, keepdims=True)
            col_lse = top + jnp.log(jnp.sum(jnp.exp(ev - top), axis=0, keepdims=True))
            b_ref[:, cs] = (-shrink * EPS * col_lse) * (1.0 / EPS) + lb_ref[:, cs]
        rg = ROW_GROUP
        while rows % rg:
            rg //= 2

        def row_group(r, carry):
            rs = pl.ds(pl.multiple_of(r * rg, rg), rg)
            m = jnp.full((rg, WIDTH), -jnp.inf, jnp.float32)
            for j in range(chunks):
                cs = slice(j * WIDTH, (j + 1) * WIDTH)
                m = jnp.maximum(m, b_ref[:, cs] - c_ref[rs, cs])
            peak = jnp.max(m, axis=1, keepdims=True)
            s = jnp.zeros((rg, WIDTH), jnp.float32)
            for j in range(chunks):
                cs = slice(j * WIDTH, (j + 1) * WIDTH)
                s = s + jnp.exp(b_ref[:, cs] - c_ref[rs, cs] - peak)
            total = jnp.sum(s, axis=1, keepdims=True)
            pot = -shrink * EPS * (peak + jnp.log(total))
            f_ref[rs, :] = pot
            a_ref[rs, :] = jnp.broadcast_to(pot * (1.0 / EPS) + la_ref[rs, :], (rg, 128))
            if emit_w:
                for j in range(chunks):
                    cs = slice(j * WIDTH, (j + 1) * WIDTH)
                    e = jnp.exp(b_ref[:, cs] - c_ref[rs, cs] - peak)
                    w_ref[rs, cs] = (e / total).astype(w_ref.dtype)
                fl_ref[:, rs] = jnp.transpose(jnp.broadcast_to(pot, (rg, 128)))[0:1, :]
                p_ref[:, rs] = lax.dot_general(
                    handed_ref[...], w_ref[rs, :], (((1,), (1,)), ((), ())),
                    preferred_element_type=jnp.float32,
                )
            return carry
        lax.fori_loop(0, rows // rg, row_group, 0)
    else:
        a_ref[...] = jnp.broadcast_to(la_ref[...], a_ref.shape)

    if do_col:
        def col_chunk(j, carry):
            cs = pl.ds(pl.multiple_of(j * WIDTH, WIDTH), WIDTH)
            shifts = [jnp.tile(a_ref[r * GROUP:(r + 1) * GROUP, :], (1, WIDTH // 128))
                      for r in range(groups)]
            m = [jnp.full((GROUP, WIDTH), -jnp.inf, jnp.float32) for _ in range(2)]
            for r in range(groups):
                m[r % 2] = jnp.maximum(m[r % 2], shifts[r] - c_ref[r * GROUP:(r + 1) * GROUP, cs])
            peak = jnp.max(jnp.maximum(m[0], m[1]), axis=0, keepdims=True)
            s = [jnp.zeros((GROUP, WIDTH), jnp.float32) for _ in range(2)]
            for r in range(groups):
                s[r % 2] = s[r % 2] + jnp.exp(shifts[r] - c_ref[r * GROUP:(r + 1) * GROUP, cs] - peak)
            lse_ref[:, cs] = peak + jnp.log(jnp.sum(s[0] + s[1], axis=0, keepdims=True))
            return carry
        lax.fori_loop(0, chunks, col_chunk, 0)


def sweep(scaled_cost, every, log_b, log_a, shrink, do_row, do_col, emit_w, handed=None):
    rows, cols = scaled_cost.shape
    outs = []
    if do_row:
        outs.append(jax.ShapeDtypeStruct((rows, 1), jnp.float32))
    if do_col:
        outs.append(jax.ShapeDtypeStruct((1, cols), jnp.float32))
    if emit_w:
        outs.append(jax.ShapeDtypeStruct((rows, cols), jnp.bfloat16))
        outs.append(jax.ShapeDtypeStruct((handed.shape[0], rows), jnp.float32))
        outs.append(jax.ShapeDtypeStruct((1, rows), jnp.float32))
    passes = (2 if do_row else 0) + (2 if do_col else 0) + (1 if emit_w else 0)
    vmem = pl.BlockSpec(memory_space=pltpu.VMEM)
    return pl.pallas_call(
        functools.partial(sweep_kernel, do_row, do_col, emit_w, shrink),
        out_shape=tuple(outs),
        in_specs=[vmem] * (5 if emit_w else 4),
        out_specs=tuple([vmem] * len(outs)),
        scratch_shapes=[pltpu.VMEM((rows, 128), jnp.float32), pltpu.VMEM((1, cols), jnp.float32)],
        compiler_params=pltpu.CompilerParams(vmem_limit_bytes=24 * 1024 * 1024),
        cost_estimate=pl.CostEstimate(
            flops=4 * passes * rows * cols,
            transcendentals=passes * rows * cols // 2,
            bytes_accessed=4 * rows * cols + (2 * rows * cols if emit_w else 0),
        ),
    )(scaled_cost, every, log_b[None, :], log_a[:, None], *([handed] if emit_w else []))


def shifted(shard, axis, by):
    devices = lax.axis_size(axis)
    pairs = [(i, i + by) for i in range(devices) if 0 <= i + by < devices]
    return lax.ppermute(shard, axis, pairs)


def local(src_cells, final_cells, growth, live, final_fates):
    pair_count = lax.axis_size("pair")
    tgt_count = lax.axis_size("tgt")
    pair_rank = lax.axis_index("pair")
    src_rank = lax.axis_index("src")
    tgt_rank = lax.axis_index("tgt")
    shrink = LAM / (LAM + EPS)
    source_all = src_cells[0]
    dims = source_all.shape[0]
    src_width = source_all.shape[1]
    rows = src_width // tgt_count
    row_off = tgt_rank * rows
    is_last = pair_rank == pair_count - 1
    source_pos = lax.dynamic_slice_in_dim(source_all, row_off, rows, 1)
    group = lax.axis_size("src") * tgt_count
    src_count = lax.axis_size("src")
    arrived = shifted(source_all, "pair", -1)
    mine_next = lax.dynamic_slice_in_dim(arrived, row_off, rows, 1)
    fin_width = final_cells.shape[1]
    mine_final = lax.dynamic_slice_in_dim(final_cells, (src_rank * rows) % fin_width, rows, 1)
    piece = jnp.where(is_last, mine_final, mine_next)
    pieces = lax.all_gather(piece, ("src", "tgt"))
    per_fin = fin_width // rows
    final_order = [
        (b % per_fin) * tgt_count + b // per_fin if per_fin == src_count else b for b in range(group)
    ]
    if per_fin == src_count:
        final_pieces = pieces[jnp.array(final_order, dtype=jnp.int32)]
        pieces = jnp.where(is_last, final_pieces, pieces)
        target_pos = jnp.transpose(pieces, (1, 0, 2)).reshape(dims, group * rows)
    else:
        final_all = lax.all_gather(final_cells, "tgt", axis=1, tiled=True)
        target_pos = jnp.where(
            is_last, final_all, jnp.transpose(pieces, (1, 0, 2)).reshape(dims, group * rows)
        )
    cols = target_pos.shape[1]
    cross = lax.dot_general(
        source_pos,
        target_pos,
        (((0,), (0,)), ((), ())),
        precision=lax.Precision.HIGHEST,
        preferred_element_type=jnp.float32,
    )
    src_sq = jnp.sum(source_pos * source_pos, axis=0)
    tgt_sq = jnp.sum(target_pos * target_pos, axis=0)
    cost_tile = (src_sq[:, None] + tgt_sq[None, :] - 2.0 * cross) / (2.0 * dims)
    live_now = lax.dynamic_index_in_dim(live, pair_rank, keepdims=False)
    live_next = lax.dynamic_index_in_dim(live, pair_rank + 1, keepdims=False)
    row_index = src_rank * src_width + row_off + jnp.arange(rows, dtype=jnp.int32)
    col_index = jnp.arange(cols, dtype=jnp.int32)
    live_src = row_index < live_now
    live_tgt = col_index < live_next
    growth_rows = lax.dynamic_slice_in_dim(growth[0], row_off, rows, 0)
    log_mass_a = jnp.where(
        live_src, jnp.log(growth_rows) - jnp.log(live_now.astype(jnp.float32)), NEG
    )
    log_mass_b = jnp.where(
        live_tgt, -jnp.log(live_next.astype(jnp.float32)) * jnp.ones((cols,), jnp.float32), NEG
    )
    scaled_cost = cost_tile * (1.0 / EPS)
    fin_fates = final_fates.astype(jnp.bfloat16)
    if tgt_count <= 4:
        got = [fin_fates] + [
            lax.ppermute(fin_fates, "tgt", [(i, (i + k) % tgt_count) for i in range(tgt_count)])
            for k in range(1, tgt_count)
        ]
        order = (tgt_rank - jnp.arange(tgt_count, dtype=jnp.int32)) % tgt_count
        got = jnp.take(jnp.stack(got), order, axis=0)
        final_handed = jnp.transpose(got, (1, 0, 2)).reshape(fin_fates.shape[0], tgt_count * fin_width)
    else:
        final_handed = lax.all_gather(fin_fates, "tgt", axis=1, tiled=True)
    fates_count = final_handed.shape[0]
    fates_pad = -fates_count % 16
    handed_pad = jnp.concatenate(
        [final_handed, jnp.zeros((fates_pad, final_handed.shape[1]), jnp.bfloat16)], axis=0
    )
    (part_lse,) = sweep(scaled_cost, log_mass_b[None, :], log_mass_b, log_mass_a, shrink, False, True, False)
    for step_num in range(ITERS):
        every = lax.all_gather(part_lse[0], ("src", "tgt"))
        if step_num + 1 < ITERS:
            pot_col, part_lse = sweep(scaled_cost, every, log_mass_b, log_mass_a, shrink, True, True, False)
        else:
            pot_col, weights, first_pull, pot_lanes = sweep(
                scaled_cost, every, log_mass_b, log_mass_a, shrink, True, False, True, handed_pad
            )
    pot_src = pot_col.reshape(rows)
    handed = jnp.where(is_last, final_handed, jnp.zeros(final_handed.shape, jnp.bfloat16))
    fate_maps = jnp.zeros((final_fates.shape[0], rows), jnp.float32)
    for section_num in range(pair_count):
        active = pair_count - 1 - section_num
        if section_num == 0:
            pulled = first_pull[:fates_count]
        else:
            pulled = lax.dot_general(
                weights, handed, (((1,), (1,)), ((), ())), preferred_element_type=jnp.float32
            ).T
        pulled = jnp.where(live_src[None, :], pulled, 0.0)
        fate_maps = jnp.where(pair_rank == active, pulled, fate_maps)
        if section_num + 1 < pair_count:
            passed = shifted(pulled.astype(jnp.bfloat16), "pair", -1)
            fresh = lax.all_gather(passed, ("src", "tgt"), axis=1, tiled=True)
            handed = jnp.where(pair_rank == active - 1, fresh, handed)
    pot_row = pot_lanes.reshape(rows)
    if tgt_count <= 4:
        got = [pot_row] + [
            lax.ppermute(pot_row, "tgt", [(i, (i + k) % tgt_count) for i in range(tgt_count)])
            for k in range(1, tgt_count)
        ]
        order = (tgt_rank - jnp.arange(tgt_count, dtype=jnp.int32)) % tgt_count
        pot_all = jnp.take(jnp.stack(got), order, axis=0).reshape(tgt_count * rows)
    else:
        pot_all = lax.all_gather(pot_row, "tgt", axis=0, tiled=True)
    return (fate_maps[None], pot_all[None])


def solution(mesh):
    placed = (P("pair", None, "src"), P(None, "tgt"), P("pair", "src"), P(), P(None, "tgt"))
    return jax.shard_map(
        local,
        mesh=mesh,
        in_specs=placed,
        out_specs=(P("pair", None, ("src", "tgt")), P("pair", "src")),
        check_vma=False,
    )
```

```python
import jax
import jax.numpy as jnp
from jax import lax
from jax.sharding import PartitionSpec as P
import functools
from jax.experimental import pallas as pl
from jax.experimental.pallas import tpu as pltpu

ITERS = 8


EPS = 0.1
LAM = 1.0
NEG = -1e30


GROUP = 32
ROW_GROUP = 128
WIDTH = 512


def sweep_kernel(do_row, do_col, emit_w, shrink, c_ref, every_ref, lb_ref, la_ref, *rest):
    rest = list(rest)
    handed_ref = rest.pop(0) if emit_w else None
    f_ref = rest.pop(0) if do_row else None
    lse_ref = rest.pop(0) if do_col else None
    w_ref = rest.pop(0) if emit_w else None
    p_ref = rest.pop(0) if emit_w else None
    fl_ref = rest.pop(0) if emit_w else None
    a_ref, b_ref = rest
    rows, cols = c_ref.shape
    groups = rows // GROUP
    chunks = cols // WIDTH

    if do_row:
        for j in range(chunks):
            cs = slice(j * WIDTH, (j + 1) * WIDTH)
            ev = every_ref[:, cs]
            top = jnp.max(ev, axis=0, keepdims=True)
            col_lse = top + jnp.log(jnp.sum(jnp.exp(ev - top), axis=0, keepdims=True))
            b_ref[:, cs] = (-shrink * EPS * col_lse) * (1.0 / EPS) + lb_ref[:, cs]
        rg = ROW_GROUP
        while rows % rg:
            rg //= 2

        def row_group(r, carry):
            rs = pl.ds(pl.multiple_of(r * rg, rg), rg)
            m = jnp.full((rg, WIDTH), -jnp.inf, jnp.float32)
            for j in range(chunks):
                cs = slice(j * WIDTH, (j + 1) * WIDTH)
                m = jnp.maximum(m, b_ref[:, cs] - c_ref[rs, cs])
            peak = jnp.max(m, axis=1, keepdims=True)
            s = jnp.zeros((rg, WIDTH), jnp.float32)
            for j in range(chunks):
                cs = slice(j * WIDTH, (j + 1) * WIDTH)
                s = s + jnp.exp(b_ref[:, cs] - c_ref[rs, cs] - peak)
            total = jnp.sum(s, axis=1, keepdims=True)
            pot = -shrink * EPS * (peak + jnp.log(total))
            f_ref[rs, :] = pot
            a_ref[rs, :] = jnp.broadcast_to(pot * (1.0 / EPS) + la_ref[rs, :], (rg, 128))
            if emit_w:
                for j in range(chunks):
                    cs = slice(j * WIDTH, (j + 1) * WIDTH)
                    e = jnp.exp(b_ref[:, cs] - c_ref[rs, cs] - peak)
                    w_ref[rs, cs] = (e / total).astype(w_ref.dtype)
                fl_ref[:, rs] = jnp.transpose(jnp.broadcast_to(pot, (rg, 128)))[0:1, :]
                p_ref[:, rs] = lax.dot_general(
                    handed_ref[...], w_ref[rs, :], (((1,), (1,)), ((), ())),
                    preferred_element_type=jnp.float32,
                )
            return carry
        lax.fori_loop(0, rows // rg, row_group, 0)
    else:
        a_ref[...] = jnp.broadcast_to(la_ref[...], a_ref.shape)

    if do_col:
        def col_chunk(j, carry):
            cs = pl.ds(pl.multiple_of(j * WIDTH, WIDTH), WIDTH)
            shifts = [jnp.tile(a_ref[r * GROUP:(r + 1) * GROUP, :], (1, WIDTH // 128))
                      for r in range(groups)]
            m = [jnp.full((GROUP, WIDTH), -jnp.inf, jnp.float32) for _ in range(2)]
            for r in range(groups):
                m[r % 2] = jnp.maximum(m[r % 2], shifts[r] - c_ref[r * GROUP:(r + 1) * GROUP, cs])
            peak = jnp.max(jnp.maximum(m[0], m[1]), axis=0, keepdims=True)
            s = [jnp.zeros((GROUP, WIDTH), jnp.float32) for _ in range(2)]
            for r in range(groups):
                s[r % 2] = s[r % 2] + jnp.exp(shifts[r] - c_ref[r * GROUP:(r + 1) * GROUP, cs] - peak)
            lse_ref[:, cs] = peak + jnp.log(jnp.sum(s[0] + s[1], axis=0, keepdims=True))
            return carry
        lax.fori_loop(0, chunks, col_chunk, 0)


def sweep(scaled_cost, every, log_b, log_a, shrink, do_row, do_col, emit_w, handed=None):
    rows, cols = scaled_cost.shape
    outs = []
    if do_row:
        outs.append(jax.ShapeDtypeStruct((rows, 1), jnp.float32))
    if do_col:
        outs.append(jax.ShapeDtypeStruct((1, cols), jnp.float32))
    if emit_w:
        outs.append(jax.ShapeDtypeStruct((rows, cols), jnp.bfloat16))
        outs.append(jax.ShapeDtypeStruct((handed.shape[0], rows), jnp.float32))
        outs.append(jax.ShapeDtypeStruct((1, rows), jnp.float32))
    passes = (2 if do_row else 0) + (2 if do_col else 0) + (1 if emit_w else 0)
    vmem = pl.BlockSpec(memory_space=pltpu.VMEM)
    return pl.pallas_call(
        functools.partial(sweep_kernel, do_row, do_col, emit_w, shrink),
        out_shape=tuple(outs),
        in_specs=[vmem] * (5 if emit_w else 4),
        out_specs=tuple([vmem] * len(outs)),
        scratch_shapes=[pltpu.VMEM((rows, 128), jnp.float32), pltpu.VMEM((1, cols), jnp.float32)],
        compiler_params=pltpu.CompilerParams(vmem_limit_bytes=24 * 1024 * 1024),
        cost_estimate=pl.CostEstimate(
            flops=4 * passes * rows * cols,
            transcendentals=passes * rows * cols // 2,
            bytes_accessed=4 * rows * cols + (2 * rows * cols if emit_w else 0),
        ),
    )(scaled_cost, every, log_b[None, :], log_a[:, None], *([handed] if emit_w else []))


def shifted(shard, axis, by):
    devices = lax.axis_size(axis)
    pairs = [(i, i + by) for i in range(devices) if 0 <= i + by < devices]
    return lax.ppermute(shard, axis, pairs)


def local(src_cells, final_cells, growth, live, final_fates):
    pair_count = lax.axis_size("pair")
    tgt_count = lax.axis_size("tgt")
    pair_rank = lax.axis_index("pair")
    src_rank = lax.axis_index("src")
    tgt_rank = lax.axis_index("tgt")
    shrink = LAM / (LAM + EPS)
    source_all = src_cells[0]
    dims = source_all.shape[0]
    src_width = source_all.shape[1]
    rows = src_width // tgt_count
    row_off = tgt_rank * rows
    is_last = pair_rank == pair_count - 1
    source_pos = lax.dynamic_slice_in_dim(source_all, row_off, rows, 1)
    group = lax.axis_size("src") * tgt_count
    src_count = lax.axis_size("src")
    mine_next = shifted(source_pos, "pair", -1)
    fin_width = final_cells.shape[1]
    mine_final = lax.dynamic_slice_in_dim(final_cells, (src_rank * rows) % fin_width, rows, 1)
    piece = jnp.where(is_last, mine_final, mine_next)
    pieces = lax.all_gather(piece, ("src", "tgt"))
    per_fin = fin_width // rows
    final_order = [
        (b % per_fin) * tgt_count + b // per_fin if per_fin == src_count else b for b in range(group)
    ]
    if per_fin == src_count:
        final_pieces = pieces[jnp.array(final_order, dtype=jnp.int32)]
        pieces = jnp.where(is_last, final_pieces, pieces)
        target_pos = jnp.transpose(pieces, (1, 0, 2)).reshape(dims, group * rows)
    else:
        final_all = lax.all_gather(final_cells, "tgt", axis=1, tiled=True)
        target_pos = jnp.where(
            is_last, final_all, jnp.transpose(pieces, (1, 0, 2)).reshape(dims, group * rows)
        )
    cols = target_pos.shape[1]
    cross = lax.dot_general(
        source_pos,
        target_pos,
        (((0,), (0,)), ((), ())),
        precision=lax.Precision.HIGHEST,
        preferred_element_type=jnp.float32,
    )
    src_sq = jnp.sum(source_pos * source_pos, axis=0)
    tgt_sq = jnp.sum(target_pos * target_pos, axis=0)
    cost_tile = (src_sq[:, None] + tgt_sq[None, :] - 2.0 * cross) / (2.0 * dims)
    live_now = lax.dynamic_index_in_dim(live, pair_rank, keepdims=False)
    live_next = lax.dynamic_index_in_dim(live, pair_rank + 1, keepdims=False)
    row_index = src_rank * src_width + row_off + jnp.arange(rows, dtype=jnp.int32)
    col_index = jnp.arange(cols, dtype=jnp.int32)
    live_src = row_index < live_now
    live_tgt = col_index < live_next
    growth_rows = lax.dynamic_slice_in_dim(growth[0], row_off, rows, 0)
    log_mass_a = jnp.where(
        live_src, jnp.log(growth_rows) - jnp.log(live_now.astype(jnp.float32)), NEG
    )
    log_mass_b = jnp.where(
        live_tgt, -jnp.log(live_next.astype(jnp.float32)) * jnp.ones((cols,), jnp.float32), NEG
    )
    scaled_cost = cost_tile * (1.0 / EPS)
    fin_fates = final_fates.astype(jnp.bfloat16)
    if tgt_count <= 4:
        got = [fin_fates] + [
            lax.ppermute(fin_fates, "tgt", [(i, (i + k) % tgt_count) for i in range(tgt_count)])
            for k in range(1, tgt_count)
        ]
        order = (tgt_rank - jnp.arange(tgt_count, dtype=jnp.int32)) % tgt_count
        got = jnp.take(jnp.stack(got), order, axis=0)
        final_handed = jnp.transpose(got, (1, 0, 2)).reshape(fin_fates.shape[0], tgt_count * fin_width)
    else:
        final_handed = lax.all_gather(fin_fates, "tgt", axis=1, tiled=True)
    fates_count = final_handed.shape[0]
    fates_pad = -fates_count % 16
    handed_pad = jnp.concatenate(
        [final_handed, jnp.zeros((fates_pad, final_handed.shape[1]), jnp.bfloat16)], axis=0
    )
    (part_lse,) = sweep(scaled_cost, log_mass_b[None, :], log_mass_b, log_mass_a, shrink, False, True, False)
    for step_num in range(ITERS):
        every = lax.all_gather(part_lse[0], ("src", "tgt"))
        if step_num + 1 < ITERS:
            pot_col, part_lse = sweep(scaled_cost, every, log_mass_b, log_mass_a, shrink, True, True, False)
        else:
            pot_col, weights, first_pull, pot_lanes = sweep(
                scaled_cost, every, log_mass_b, log_mass_a, shrink, True, False, True, handed_pad
            )
    pot_src = pot_col.reshape(rows)
    handed = jnp.where(is_last, final_handed, jnp.zeros(final_handed.shape, jnp.bfloat16))
    fate_maps = jnp.zeros((final_fates.shape[0], rows), jnp.float32)
    for section_num in range(pair_count):
        active = pair_count - 1 - section_num
        if section_num == 0:
            pulled = first_pull[:fates_count]
        else:
            pulled = lax.dot_general(
                weights, handed, (((1,), (1,)), ((), ())), preferred_element_type=jnp.float32
            ).T
        pulled = jnp.where(live_src[None, :], pulled, 0.0)
        fate_maps = jnp.where(pair_rank == active, pulled, fate_maps)
        if section_num + 1 < pair_count:
            passed = shifted(pulled.astype(jnp.bfloat16), "pair", -1)
            fresh = lax.all_gather(passed, ("src", "tgt"), axis=1, tiled=True)
            handed = jnp.where(pair_rank == active - 1, fresh, handed)
    pot_row = pot_lanes.reshape(rows)
    if tgt_count <= 4:
        got = [pot_row] + [
            lax.ppermute(pot_row, "tgt", [(i, (i + k) % tgt_count) for i in range(tgt_count)])
            for k in range(1, tgt_count)
        ]
        order = (tgt_rank - jnp.arange(tgt_count, dtype=jnp.int32)) % tgt_count
        pot_all = jnp.take(jnp.stack(got), order, axis=0).reshape(tgt_count * rows)
    else:
        pot_all = lax.all_gather(pot_row, "tgt", axis=0, tiled=True)
    return (fate_maps[None], pot_all[None])


def solution(mesh):
    placed = (P("pair", None, "src"), P(None, "tgt"), P("pair", "src"), P(), P(None, "tgt"))
    return jax.shard_map(
        local,
        mesh=mesh,
        in_specs=placed,
        out_specs=(P("pair", None, ("src", "tgt")), P("pair", "src")),
        check_vma=False,
    )
```
